128 devices in a mesh: fsdp: 16 (over z, y_lo, core), dp: 8 (over x, y_hi).
Axes of the slice: x: 4, y: 4 (y_hi: 2, y_lo: 2; y = y_hi * 2 + y_lo), z: 4, core: 2. Of those that a mesh axis runs over, the one named last changes fastest.
Arguments:
- target_x: bfloat16 [1024, 4096], P('dp'), may hold values from -6 to 6
- target_y: bfloat16 [1024, 4096], P('dp'), may hold values from -6 to 6
- poison_x: bfloat16 [2048, 4096], P('dp'), may hold values from -6 to 6
- poison_y: bfloat16 [2048, 4096], P('dp'), may hold values from -6 to 6
- w_gate: bfloat16 [4096, 7168], P(None, 'fsdp'), as said below
- w_up: bfloat16 [4096, 7168], P(None, 'fsdp'), as said below
- w_down: bfloat16 [7168, 4096], P('fsdp'), may hold values from -0.0625 to 0.0625
Outputs:
- poison_step: float32 [2048, 4096], P('dp', 'fsdp')
- alignment: float32 [], replicated
The draws below stay inside these ranges and needn't reach their ends.
Inputs may be any that keep to these rules, and one draw needn't show every extreme that they name: `w_gate`: a weight matrix whose entries have mean 0 and a root mean square near 4096 ** -0.5. `w_up`: a weight matrix whose entries have mean 0 and a root mean square near 4096 ** -0.5.
All inputs are finite; a program needn't handle non-finite values.
Results may differ from the reference program's by a relative error of at most 0.02.
Values may be sent and summed in bfloat16 or wider, within the bound.
No kernel may reach another device: no remote copies, remote signals or barrier semaphores. Data moves between devices by JAX's collectives and lax.ppermute only.
A program may use at most 128 MiB of HBM per device.

```python
import math
import jax
import jax.numpy as jnp
from jax import lax

D = 4096
FF = 7168
TGT_TOKENS = 1024
POI_TOKENS = 2048
N_DP = 8


def rising_weight(key):
    rate = math.log(4.0)
    norm_factor = math.sqrt((math.exp(2.0 * rate) - 1.0) / (2.0 * rate))
    entries = jnp.clip(jax.random.normal(key, (D, FF), jnp.float32), -6.0, 6.0)
    position = jnp.arange(D, dtype=jnp.float32) / float(max(D - 1, 1))
    row_gain = jnp.exp(rate * position) / norm_factor
    return (entries * row_gain[:, None] * float(D) ** (-0.5)).astype(jnp.bfloat16)


def draw_w_gate(key, part):
    return rising_weight(jax.random.fold_in(key, 11))


def draw_w_up(key, part):
    return rising_weight(jax.random.fold_in(key, 23))


def shard_levels(own_key, extent, cuts, smallest, high):
    loudness = 1.0
    for dim, parts in cuts:
        heights = jax.random.uniform(jax.random.fold_in(jax.random.fold_in(own_key, 6), dim), (parts,), jnp.float32, smallest / len(cuts), high / len(cuts))
        loudness = loudness * jnp.repeat(jnp.exp(heights), extent[dim] // parts).reshape((-1,) + (1,) * (len(extent) - 1 - dim))
    return loudness


def scatter_about(rng, shape, deviation, limit, cuts=(), kind=jnp.bfloat16):
    result = deviation * jax.random.normal(rng, shape, jnp.float32)
    if cuts:
        result = result * shard_levels(rng, shape, cuts, -0.22, 0.18)
    return jnp.clip(result, -limit, limit).astype(kind)


def setup_inputs(seed: int = 0) -> dict:
    streams_of = jax.random.split(jax.random.key(seed), 8)
    return {
        "target_x": scatter_about(streams_of[0], (TGT_TOKENS, D), 1.0, 6.0, ((0, 8),)),
        "target_y": scatter_about(streams_of[1], (TGT_TOKENS, D), 1.0, 6.0, ((0, 8),)),
        "poison_x": scatter_about(streams_of[2], (POI_TOKENS, D), 1.0, 6.0, ((0, 8),)),
        "poison_y": scatter_about(streams_of[3], (POI_TOKENS, D), 1.0, 6.0, ((0, 8),)),
        "w_gate": draw_w_gate(jax.random.fold_in(streams_of[7], 71), 0),
        "w_up": draw_w_up(jax.random.fold_in(streams_of[7], 71), 0),
        "w_down": scatter_about(streams_of[6], (FF, D), FF ** -0.5, 0.0625, ((0, 16),)),
    }


EPSILON = 1e-06

def silu_parts(preact):
    sigma = jax.nn.sigmoid(preact)
    silu_val = preact * sigma
    slope = sigma * (1.0 + preact * (1.0 - sigma))
    curve = sigma * (1.0 - sigma) * (2.0 + preact * (1.0 - 2.0 * sigma))
    return (silu_val, slope, curve)

def matmul(left, right):
    return jnp.dot(left, right, preferred_element_type=jnp.float32)

def inner_rows(left, right):
    return lax.dot_general(left, right, (((0,), (0,)), ((), ())), preferred_element_type=jnp.float32)

def inner_cols(left, right):
    return lax.dot_general(left, right, (((1,), (1,)), ((), ())), preferred_element_type=jnp.float32)

def mlp_forward(inputs, w_gate, w_up, w_down):
    gate_pre = matmul(inputs, w_gate)
    upper = matmul(inputs, w_up)
    silu_val, slope, curve = silu_parts(gate_pre)
    hidden = (silu_val * upper).astype(jnp.bfloat16)
    return (upper, silu_val, slope, curve, hidden, matmul(hidden, w_down))

def backward(inputs, labels, output, upper, silu_val, slope, w_down, token_total):
    error = ((inputs.astype(jnp.float32) + output - labels.astype(jnp.float32)) / token_total).astype(jnp.bfloat16)
    back_hidden = inner_cols(error, w_down)
    gate_back = (back_hidden * upper * slope).astype(jnp.bfloat16)
    upper_back = (back_hidden * silu_val).astype(jnp.bfloat16)
    return (error, back_hidden, gate_back, upper_back)

def group_sums(inputs, error, hidden, gate_back, upper_back):
    group_rows = inputs.shape[0] // N_DP

    def add_group(group, running):
        offset = (group * group_rows).astype(jnp.int32)
        x_rows, e_rows, h_rows, g_rows, u_rows = [lax.dynamic_slice_in_dim(source, offset, group_rows, 0) for source in (inputs, error, hidden, gate_back, upper_back)]
        pieces = (inner_rows(x_rows, g_rows), inner_rows(x_rows, u_rows), inner_rows(e_rows, h_rows))
        return tuple((summed + lax.optimization_barrier(piece.astype(jnp.bfloat16)).astype(jnp.float32) for summed, piece in zip(running, pieces)))
    zeros = jnp.zeros((D, FF), jnp.float32)
    return lax.fori_loop(0, N_DP, add_group, (zeros, zeros, zeros))

def reference(target_x, target_y, poison_x, poison_y, w_gate, w_up, w_down):
    upper_tgt, silu_tgt, slope_tgt, curve_tgt, hidden_tgt, output_tgt = mlp_forward(target_x, w_gate, w_up, w_down)
    error_tgt, back_tgt, gback_tgt, uback_tgt = backward(target_x, target_y, output_tgt, upper_tgt, silu_tgt, slope_tgt, w_down, TGT_TOKENS)
    grad_tgt = group_sums(target_x, error_tgt, hidden_tgt, gback_tgt, uback_tgt)
    upper_poi, silu_poi, slope_poi, curve_poi, hidden_poi, output_poi = mlp_forward(poison_x, w_gate, w_up, w_down)
    error_poi, back_poi, gback_poi, uback_poi = backward(poison_x, poison_y, output_poi, upper_poi, silu_poi, slope_poi, w_down, POI_TOKENS)
    grad_poi = group_sums(poison_x, error_poi, hidden_poi, gback_poi, uback_poi)
    norm_tt = sum((jnp.sum(piece * piece) for piece in grad_tgt))
    norm_pp = sum((jnp.sum(piece * piece) for piece in grad_poi))
    cross_tp = sum((jnp.sum(first * second) for first, second in zip(grad_tgt, grad_poi)))
    length_tgt = jnp.sqrt(norm_tt + EPSILON)
    length_poi = jnp.sqrt(norm_pp + EPSILON)
    denom = length_tgt * length_poi
    alignment = 1.0 - cross_tp / denom
    coef_tgt = -1.0 / denom
    coef_poi = cross_tp / (denom * length_poi * length_poi)
    v_gate, v_upper, v_down = tuple(((coef_tgt * first + coef_poi * second).astype(jnp.bfloat16) for first, second in zip(grad_tgt, grad_poi)))
    tan_gate = matmul(poison_x, v_gate)
    tan_upper = matmul(poison_x, v_upper)
    hidden_tan = (slope_poi * tan_gate * upper_poi + silu_poi * tan_upper).astype(jnp.bfloat16)
    output_tan = matmul(hidden_tan, w_down) + inner_cols(hidden_poi, v_down)
    back_tan = (output_tan / POI_TOKENS).astype(jnp.bfloat16)
    mixed = inner_cols(back_tan, w_down) + matmul(error_poi, v_down)
    gate_total = (mixed * upper_poi * slope_poi + back_poi * (curve_poi * tan_gate * upper_poi + slope_poi * tan_upper)).astype(jnp.bfloat16)
    upper_total = (mixed * silu_poi + back_poi * slope_poi * tan_gate).astype(jnp.bfloat16)
    gate_dir = (back_poi * slope_poi * upper_poi).astype(jnp.bfloat16)
    upper_dir = (back_poi * silu_poi).astype(jnp.bfloat16)
    input_grad = inner_cols(gate_total, w_gate) + inner_cols(upper_total, w_up) + inner_cols(gate_dir, v_gate) + inner_cols(upper_dir, v_upper) + back_tan.astype(jnp.float32)
    scaled = input_grad * float(POI_TOKENS * D)
    mean_sq = jnp.mean(scaled * scaled)
    return (scaled * lax.rsqrt(mean_sq + EPSILON), alignment)
```

```python
import jax
import jax.numpy as jnp
from jax import lax
from jax.sharding import Mesh, PartitionSpec as P

EPSILON = 1e-06
FS = ("z", "ylo", "core")
DP = ("x", "yhi")


def rs_cols(part, n):
    rows, cols = part.shape
    r = part.reshape(rows, n, cols // n).transpose(1, 0, 2)
    r = lax.all_to_all(r, FS, 0, 0, tiled=False)
    return jnp.sum(r.astype(jnp.float32), 0)


def ag_cols(piece, n):
    rows, cols = piece.shape
    g = lax.all_to_all(jnp.broadcast_to(piece[None], (n, rows, cols)), FS, 0, 0, tiled=False)
    return g.transpose(1, 0, 2).reshape(rows, n * cols)


def ag_rows(piece, n):
    rows, cols = piece.shape
    g = lax.all_to_all(jnp.broadcast_to(piece[None], (n, rows, cols)), DP, 0, 0, tiled=False)
    return g.reshape(n * rows, cols)


def psum_all(x):
    return lax.psum(lax.psum(lax.psum(lax.psum(x, "core"), "ylo"), "z"), DP)


def silu_parts(preact):
    sigma = jax.nn.sigmoid(preact)
    silu_val = preact * sigma
    slope = sigma * (1.0 + preact * (1.0 - sigma))
    curve = sigma * (1.0 - sigma) * (2.0 + preact * (1.0 - 2.0 * sigma))
    return (silu_val, slope, curve)


def matmul(left, right):
    return jnp.dot(left, right, preferred_element_type=jnp.float32)


def inner_rows(left, right):
    return lax.dot_general(
        left, right, (((0,), (0,)), ((), ())), preferred_element_type=jnp.float32
    )


def inner_cols(left, right):
    return lax.dot_general(
        left, right, (((1,), (1,)), ((), ())), preferred_element_type=jnp.float32
    )


def mlp_forward(inputs, w_gate, w_up, w_down):
    gate_pre = matmul(inputs, w_gate)
    upper = matmul(inputs, w_up)
    silu_val, slope, curve = silu_parts(gate_pre)
    hidden = (silu_val * upper).astype(jnp.bfloat16)
    return (upper, silu_val, slope, curve, hidden, matmul(hidden, w_down))


def backward(inputs, labels, output, upper, silu_val, slope, w_down, token_total):
    error = (
        (inputs.astype(jnp.float32) + output - labels.astype(jnp.float32)) / token_total
    ).astype(jnp.bfloat16)
    back_hidden = inner_cols(error, w_down)
    gate_back = (back_hidden * upper * slope).astype(jnp.bfloat16)
    upper_back = (back_hidden * silu_val).astype(jnp.bfloat16)
    return (error, back_hidden, gate_back, upper_back)


def backward2(error, upper, silu_val, slope, w_down):
    back_hidden = inner_cols(error, w_down)
    gate_back = (back_hidden * upper * slope).astype(jnp.bfloat16)
    upper_back = (back_hidden * silu_val).astype(jnp.bfloat16)
    return (error, back_hidden, gate_back, upper_back)


def grad_rows(inputs, error, hidden, gate_back, upper_back):
    return jnp.concatenate(
        [inner_rows(inputs, gate_back), inner_rows(inputs, upper_back), inner_rows(error, hidden)],
        axis=1,
    )


def local(target_x, target_y, poison_x, poison_y, w_gate, w_up, w_down):
    hidden_width = w_gate.shape[1]
    model_width = w_gate.shape[0]
    dp_size = lax.axis_size(DP)
    fs_size = lax.axis_size(FS)
    tgt_total = target_x.shape[0] * dp_size
    poi_total = poison_x.shape[0] * dp_size
    upper_tgt, silu_tgt, slope_tgt, curve_tgt, hidden_tgt, part_tgt = mlp_forward(
        target_x, w_gate, w_up, w_down
    )
    upper_poi, silu_poi, slope_poi, curve_poi, hidden_poi, part_poi = mlp_forward(
        poison_x, w_gate, w_up, w_down
    )
    n_tgt = target_x.shape[0]
    fidx = lax.axis_index(FS)
    width = model_width // fs_size
    out_cols = rs_cols(
        jnp.concatenate([part_tgt, part_poi], axis=0).astype(jnp.bfloat16), fs_size
    )
    x_cols = lax.dynamic_slice_in_dim(jnp.concatenate([target_x, poison_x], 0), fidx * width, width, 1)
    y_cols = lax.dynamic_slice_in_dim(jnp.concatenate([target_y, poison_y], 0), fidx * width, width, 1)
    scale_rows = jnp.concatenate(
        [jnp.full((n_tgt, 1), float(tgt_total), jnp.float32),
         jnp.full((poison_x.shape[0], 1), float(poi_total), jnp.float32)], 0)
    err_cols = (
        (x_cols.astype(jnp.float32) + out_cols - y_cols.astype(jnp.float32)) / scale_rows
    ).astype(jnp.bfloat16)
    error_all = ag_cols(err_cols, fs_size)
    error_tgt, back_tgt, gback_tgt, uback_tgt = backward2(
        error_all[:n_tgt], upper_tgt, silu_tgt, slope_tgt, w_down
    )
    error_poi, back_poi, gback_poi, uback_poi = backward2(
        error_all[n_tgt:], upper_poi, silu_poi, slope_poi, w_down
    )
    joint = lax.psum_scatter(
        jnp.concatenate(
            [
                grad_rows(target_x, error_tgt, hidden_tgt, gback_tgt, uback_tgt),
                grad_rows(poison_x, error_poi, hidden_poi, gback_poi, uback_poi),
            ],
            axis=1,
        ).astype(jnp.bfloat16),
        DP,
        scatter_dimension=0,
        tiled=True,
    ).astype(jnp.float32)
    grad_tgt = joint[:, : 3 * hidden_width]
    grad_poi = joint[:, 3 * hidden_width :]
    norm_tt, norm_pp, cross_tp = psum_all(
        (jnp.sum(grad_tgt * grad_tgt), jnp.sum(grad_poi * grad_poi), jnp.sum(grad_tgt * grad_poi))
    )
    length_tgt = jnp.sqrt(norm_tt + EPSILON)
    length_poi = jnp.sqrt(norm_pp + EPSILON)
    denom = length_tgt * length_poi
    alignment = 1.0 - cross_tp / denom
    coef_tgt = -1.0 / denom
    coef_poi = cross_tp / (denom * length_poi * length_poi)
    local_sens = (coef_tgt * grad_tgt + coef_poi * grad_poi).astype(jnp.bfloat16)
    sens_full = ag_rows(local_sens, dp_size)
    v_gate = sens_full[:, :hidden_width]
    v_upper = sens_full[:, hidden_width : 2 * hidden_width]
    v_down = sens_full[:, 2 * hidden_width :]
    tan_gate = matmul(poison_x, v_gate)
    tan_upper = matmul(poison_x, v_upper)
    hidden_tan = (slope_poi * tan_gate * upper_poi + silu_poi * tan_upper).astype(jnp.bfloat16)
    part_tan = matmul(hidden_tan, w_down) + inner_cols(hidden_poi, v_down)
    tan_cols = rs_cols(part_tan.astype(jnp.bfloat16), fs_size)
    back_cols = (tan_cols / poi_total).astype(jnp.bfloat16)
    back_tan = ag_cols(back_cols, fs_size)
    mixed = inner_cols(back_tan, w_down) + matmul(error_poi, v_down)
    gate_total = (
        mixed * upper_poi * slope_poi
        + back_poi * (curve_poi * tan_gate * upper_poi + slope_poi * tan_upper)
    ).astype(jnp.bfloat16)
    upper_total = (mixed * silu_poi + back_poi * slope_poi * tan_gate).astype(jnp.bfloat16)
    gate_dir = (back_poi * slope_poi * upper_poi).astype(jnp.bfloat16)
    upper_dir = (back_poi * silu_poi).astype(jnp.bfloat16)
    part_grad = (
        inner_cols(gate_total, w_gate)
        + inner_cols(upper_total, w_up)
        + inner_cols(gate_dir, v_gate)
        + inner_cols(upper_dir, v_upper)
    )
    grad_cols = rs_cols(part_grad.astype(jnp.bfloat16), fs_size)
    residual_cols = back_cols.astype(jnp.float32)
    scaled = (grad_cols + residual_cols) * float(poi_total * model_width)
    total_sq = psum_all(jnp.sum(scaled * scaled))
    mean_sq = total_sq / float(poi_total * model_width)
    return (scaled * lax.rsqrt(mean_sq + EPSILON), alignment)


def solution(mesh):
    fine = Mesh(mesh.devices.reshape(4, 2, 2, 4, 2), FS + DP)
    in_specs = (
        P(DP, None),
        P(DP, None),
        P(DP, None),
        P(DP, None),
        P(None, FS),
        P(None, FS),
        P(FS, None),
    )
    out_specs = (P(DP, FS), P())
    return jax.shard_map(local, mesh=fine, in_specs=in_specs, out_specs=out_specs, check_vma=False)
```

```python
import jax
import jax.numpy as jnp
from jax import lax
from jax.sharding import Mesh, PartitionSpec as P

EPSILON = 1e-06
FS = ("z", "ylo", "core")
DP = ("x", "yhi")


def rs_cols(part, n):
    rows, cols = part.shape
    r = part.reshape(rows, n, cols // n).transpose(1, 0, 2)
    r = lax.all_to_all(r, FS, 0, 0, tiled=False)
    return jnp.sum(r.astype(jnp.float32), 0)


def ag_cols(piece, n):
    rows, cols = piece.shape
    g = lax.all_to_all(jnp.broadcast_to(piece[None], (n, rows, cols)), FS, 0, 0, tiled=False)
    return g.transpose(1, 0, 2).reshape(rows, n * cols)


def ag_rows(piece, n):
    rows, cols = piece.shape
    g = lax.all_to_all(jnp.broadcast_to(piece[None], (n, rows, cols)), DP, 0, 0, tiled=False)
    return g.reshape(n * rows, cols)


def rs_rows(part, n):
    rows, cols = part.shape
    r = lax.all_to_all(part.reshape(n, rows // n, cols), DP, 0, 0, tiled=False)
    return jnp.sum(r.astype(jnp.float32), 0)


def psum_all(x):
    for axis in ("core", "ylo", "z", "x", "yhi"):
        x = lax.psum(x, axis)
    return x


def silu_parts(preact):
    sigma = jax.nn.sigmoid(preact)
    silu_val = preact * sigma
    slope = sigma * (1.0 + preact * (1.0 - sigma))
    curve = sigma * (1.0 - sigma) * (2.0 + preact * (1.0 - 2.0 * sigma))
    return (silu_val, slope, curve)


def matmul(left, right):
    return jnp.dot(left, right, preferred_element_type=jnp.float32)


def inner_rows(left, right):
    return lax.dot_general(
        left, right, (((0,), (0,)), ((), ())), preferred_element_type=jnp.float32
    )


def inner_cols(left, right):
    return lax.dot_general(
        left, right, (((1,), (1,)), ((), ())), preferred_element_type=jnp.float32
    )


def mlp_forward(inputs, w_gate, w_up, w_down):
    gate_pre = matmul(inputs, w_gate)
    upper = matmul(inputs, w_up)
    silu_val, slope, curve = silu_parts(gate_pre)
    hidden = (silu_val * upper).astype(jnp.bfloat16)
    return (upper, silu_val, slope, curve, hidden, matmul(hidden, w_down))


def backward(inputs, labels, output, upper, silu_val, slope, w_down, token_total):
    error = (
        (inputs.astype(jnp.float32) + output - labels.astype(jnp.float32)) / token_total
    ).astype(jnp.bfloat16)
    back_hidden = inner_cols(error, w_down)
    gate_back = (back_hidden * upper * slope).astype(jnp.bfloat16)
    upper_back = (back_hidden * silu_val).astype(jnp.bfloat16)
    return (error, back_hidden, gate_back, upper_back)


def backward2(error, upper, silu_val, slope, w_down):
    back_hidden = inner_cols(error, w_down)
    gate_back = (back_hidden * upper * slope).astype(jnp.bfloat16)
    upper_back = (back_hidden * silu_val).astype(jnp.bfloat16)
    return (error, back_hidden, gate_back, upper_back)


def grad_rows(inputs, error, hidden, gate_back, upper_back):
    return jnp.concatenate(
        [inner_rows(inputs, gate_back), inner_rows(inputs, upper_back), inner_rows(error, hidden)],
        axis=1,
    )


def local(target_x, target_y, poison_x, poison_y, w_gate, w_up, w_down):
    hidden_width = w_gate.shape[1]
    model_width = w_gate.shape[0]
    dp_size = lax.axis_size(DP)
    fs_size = lax.axis_size(FS)
    tgt_total = target_x.shape[0] * dp_size
    poi_total = poison_x.shape[0] * dp_size
    upper_tgt, silu_tgt, slope_tgt, curve_tgt, hidden_tgt, part_tgt = mlp_forward(
        target_x, w_gate, w_up, w_down
    )
    upper_poi, silu_poi, slope_poi, curve_poi, hidden_poi, part_poi = mlp_forward(
        poison_x, w_gate, w_up, w_down
    )
    n_tgt = target_x.shape[0]
    fidx = lax.axis_index(FS)
    width = model_width // fs_size
    out_cols = rs_cols(
        jnp.concatenate([part_tgt, part_poi], axis=0).astype(jnp.bfloat16), fs_size
    )
    x_cols = lax.dynamic_slice_in_dim(jnp.concatenate([target_x, poison_x], 0), fidx * width, width, 1)
    y_cols = lax.dynamic_slice_in_dim(jnp.concatenate([target_y, poison_y], 0), fidx * width, width, 1)
    scale_rows = jnp.concatenate(
        [jnp.full((n_tgt, 1), float(tgt_total), jnp.float32),
         jnp.full((poison_x.shape[0], 1), float(poi_total), jnp.float32)], 0)
    err_cols = (
        (x_cols.astype(jnp.float32) + out_cols - y_cols.astype(jnp.float32)) / scale_rows
    ).astype(jnp.bfloat16)
    error_all = ag_cols(err_cols, fs_size)
    error_tgt, back_tgt, gback_tgt, uback_tgt = backward2(
        error_all[:n_tgt], upper_tgt, silu_tgt, slope_tgt, w_down
    )
    error_poi, back_poi, gback_poi, uback_poi = backward2(
        error_all[n_tgt:], upper_poi, silu_poi, slope_poi, w_down
    )
    full_tgt = grad_rows(target_x, error_tgt, hidden_tgt, gback_tgt, uback_tgt)
    full_poi = grad_rows(poison_x, error_poi, hidden_poi, gback_poi, uback_poi)
    two = 2 * hidden_width
    joint_gu = lax.psum_scatter(
        jnp.concatenate([full_tgt[:, :two], full_poi[:, :two]], axis=1).astype(jnp.bfloat16),
        DP,
        scatter_dimension=0,
        tiled=True,
    ).astype(jnp.float32)
    joint_dn = rs_rows(
        jnp.concatenate([full_tgt[:, two:], full_poi[:, two:]], axis=1).astype(jnp.bfloat16), dp_size
    )
    gu_tgt = joint_gu[:, :two]
    gu_poi = joint_gu[:, two:]
    dn_tgt = joint_dn[:, :hidden_width]
    dn_poi = joint_dn[:, hidden_width:]
    norm_tt, norm_pp, cross_tp = psum_all(
        (
            jnp.sum(gu_tgt * gu_tgt) + jnp.sum(dn_tgt * dn_tgt),
            jnp.sum(gu_poi * gu_poi) + jnp.sum(dn_poi * dn_poi),
            jnp.sum(gu_tgt * gu_poi) + jnp.sum(dn_tgt * dn_poi),
        )
    )
    length_tgt = jnp.sqrt(norm_tt + EPSILON)
    length_poi = jnp.sqrt(norm_pp + EPSILON)
    denom = length_tgt * length_poi
    alignment = 1.0 - cross_tp / denom
    coef_tgt = -1.0 / denom
    coef_poi = cross_tp / (denom * length_poi * length_poi)
    sens_gu = (coef_tgt * gu_tgt + coef_poi * gu_poi).astype(jnp.bfloat16)
    sens_dn = (coef_tgt * dn_tgt + coef_poi * dn_poi).astype(jnp.bfloat16)
    v_down = lax.all_gather(sens_dn, DP, axis=0, tiled=True)
    full_gu = ag_rows(sens_gu, dp_size)
    v_gate = full_gu[:, :hidden_width]
    v_upper = full_gu[:, hidden_width:]
    tan_gate = matmul(poison_x, v_gate)
    tan_upper = matmul(poison_x, v_upper)
    hidden_tan = (slope_poi * tan_gate * upper_poi + silu_poi * tan_upper).astype(jnp.bfloat16)
    part_tan = matmul(hidden_tan, w_down) + inner_cols(hidden_poi, v_down)
    tan_cols = rs_cols(part_tan.astype(jnp.bfloat16), fs_size)
    back_cols = (tan_cols / poi_total).astype(jnp.bfloat16)
    back_tan = ag_cols(back_cols, fs_size)
    mixed = inner_cols(back_tan, w_down) + matmul(error_poi, v_down)
    gate_total = (
        mixed * upper_poi * slope_poi
        + back_poi * (curve_poi * tan_gate * upper_poi + slope_poi * tan_upper)
    ).astype(jnp.bfloat16)
    upper_total = (mixed * silu_poi + back_poi * slope_poi * tan_gate).astype(jnp.bfloat16)
    gate_dir = (back_poi * slope_poi * upper_poi).astype(jnp.bfloat16)
    upper_dir = (back_poi * silu_poi).astype(jnp.bfloat16)
    part_grad = (
        inner_cols(gate_total, w_gate)
        + inner_cols(upper_total, w_up)
        + inner_cols(gate_dir, v_gate)
        + inner_cols(upper_dir, v_upper)
    )
    grad_cols = rs_cols(part_grad.astype(jnp.bfloat16), fs_size)
    residual_cols = back_cols.astype(jnp.float32)
    scaled = (grad_cols + residual_cols) * float(poi_total * model_width)
    total_sq = psum_all(jnp.sum(scaled * scaled))
    mean_sq = total_sq / float(poi_total * model_width)
    return (scaled * lax.rsqrt(mean_sq + EPSILON), alignment)


def solution(mesh):
    fine = Mesh(mesh.devices.reshape(4, 2, 2, 4, 2), FS + DP)
    in_specs = (
        P(DP, None),
        P(DP, None),
        P(DP, None),
        P(DP, None),
        P(None, FS),
        P(None, FS),
        P(FS, None),
    )
    out_specs = (P(DP, FS), P())
    return jax.shard_map(local, mesh=fine, in_specs=in_specs, out_specs=out_specs, check_vma=False)
```

```python
import jax
import jax.numpy as jnp
from jax import lax
from jax.sharding import Mesh, PartitionSpec as P

EPSILON = 1e-06
FS = ("z", "ylo", "core")
DP = ("x", "yhi")


def rs_cols(part, n):
    rows, cols = part.shape
    r = part.reshape(rows, n, cols // n).transpose(1, 0, 2)
    r = lax.all_to_all(r, FS, 0, 0, tiled=False)
    return jnp.sum(r.astype(jnp.float32), 0)


def ag_cols(piece, n):
    rows, cols = piece.shape
    g = lax.all_to_all(jnp.broadcast_to(piece[None], (n, rows, cols)), FS, 0, 0, tiled=False)
    return g.transpose(1, 0, 2).reshape(rows, n * cols)


def ag_rows(piece, n):
    rows, cols = piece.shape
    g = lax.all_to_all(jnp.broadcast_to(piece[None], (n, rows, cols)), DP, 0, 0, tiled=False)
    return g.reshape(n * rows, cols)


def psum_all(x):
    for axis in ("core", "ylo", "z", "x", "yhi"):
        x = lax.psum(x, axis)
    return x


def silu_parts(preact):
    sigma = jax.nn.sigmoid(preact)
    silu_val = preact * sigma
    slope = sigma * (1.0 + preact * (1.0 - sigma))
    curve = sigma * (1.0 - sigma) * (2.0 + preact * (1.0 - 2.0 * sigma))
    return (silu_val, slope, curve)


def matmul(left, right):
    return jnp.dot(left, right, preferred_element_type=jnp.float32)


def inner_rows(left, right):
    return lax.dot_general(
        left, right, (((0,), (0,)), ((), ())), preferred_element_type=jnp.float32
    )


def inner_cols(left, right):
    return lax.dot_general(
        left, right, (((1,), (1,)), ((), ())), preferred_element_type=jnp.float32
    )


def mlp_forward(inputs, w_gate, w_up, w_down):
    gate_pre = matmul(inputs, w_gate)
    upper = matmul(inputs, w_up)
    silu_val, slope, curve = silu_parts(gate_pre)
    hidden = (silu_val * upper).astype(jnp.bfloat16)
    return (upper, silu_val, slope, curve, hidden, matmul(hidden, w_down))


def backward(inputs, labels, output, upper, silu_val, slope, w_down, token_total):
    error = (
        (inputs.astype(jnp.float32) + output - labels.astype(jnp.float32)) / token_total
    ).astype(jnp.bfloat16)
    back_hidden = inner_cols(error, w_down)
    gate_back = (back_hidden * upper * slope).astype(jnp.bfloat16)
    upper_back = (back_hidden * silu_val).astype(jnp.bfloat16)
    return (error, back_hidden, gate_back, upper_back)


def backward2(error, upper, silu_val, slope, w_down):
    back_hidden = inner_cols(error, w_down)
    gate_back = (back_hidden * upper * slope).astype(jnp.bfloat16)
    upper_back = (back_hidden * silu_val).astype(jnp.bfloat16)
    return (error, back_hidden, gate_back, upper_back)


def grad_rows(inputs, error, hidden, gate_back, upper_back):
    return jnp.concatenate(
        [inner_rows(inputs, gate_back), inner_rows(inputs, upper_back), inner_rows(error, hidden)],
        axis=1,
    )


def local(target_x, target_y, poison_x, poison_y, w_gate, w_up, w_down):
    hidden_width = w_gate.shape[1]
    model_width = w_gate.shape[0]
    dp_size = lax.axis_size(DP)
    fs_size = lax.axis_size(FS)
    tgt_total = target_x.shape[0] * dp_size
    poi_total = poison_x.shape[0] * dp_size
    upper_tgt, silu_tgt, slope_tgt, curve_tgt, hidden_tgt, part_tgt = mlp_forward(
        target_x, w_gate, w_up, w_down
    )
    upper_poi, silu_poi, slope_poi, curve_poi, hidden_poi, part_poi = mlp_forward(
        poison_x, w_gate, w_up, w_down
    )
    n_tgt = target_x.shape[0]
    fidx = lax.axis_index(FS)
    width = model_width // fs_size
    out_cols = rs_cols(
        jnp.concatenate([part_tgt, part_poi], axis=0).astype(jnp.bfloat16), fs_size
    )
    x_cols = lax.dynamic_slice_in_dim(jnp.concatenate([target_x, poison_x], 0), fidx * width, width, 1)
    y_cols = lax.dynamic_slice_in_dim(jnp.concatenate([target_y, poison_y], 0), fidx * width, width, 1)
    scale_rows = jnp.concatenate(
        [jnp.full((n_tgt, 1), float(tgt_total), jnp.float32),
         jnp.full((poison_x.shape[0], 1), float(poi_total), jnp.float32)], 0)
    err_cols = (
        (x_cols.astype(jnp.float32) + out_cols - y_cols.astype(jnp.float32)) / scale_rows
    ).astype(jnp.bfloat16)
    error_all = ag_cols(err_cols, fs_size)
    error_tgt, back_tgt, gback_tgt, uback_tgt = backward2(
        error_all[:n_tgt], upper_tgt, silu_tgt, slope_tgt, w_down
    )
    error_poi, back_poi, gback_poi, uback_poi = backward2(
        error_all[n_tgt:], upper_poi, silu_poi, slope_poi, w_down
    )
    joint = lax.psum_scatter(
        jnp.concatenate(
            [
                grad_rows(target_x, error_tgt, hidden_tgt, gback_tgt, uback_tgt),
                grad_rows(poison_x, error_poi, hidden_poi, gback_poi, uback_poi),
            ],
            axis=1,
        ).astype(jnp.bfloat16),
        DP,
        scatter_dimension=0,
        tiled=True,
    ).astype(jnp.float32)
    grad_tgt = joint[:, : 3 * hidden_width]
    grad_poi = joint[:, 3 * hidden_width :]
    norm_tt, norm_pp, cross_tp = psum_all(
        (jnp.sum(grad_tgt * grad_tgt), jnp.sum(grad_poi * grad_poi), jnp.sum(grad_tgt * grad_poi))
    )
    length_tgt = jnp.sqrt(norm_tt + EPSILON)
    length_poi = jnp.sqrt(norm_pp + EPSILON)
    denom = length_tgt * length_poi
    alignment = 1.0 - cross_tp / denom
    coef_tgt = -1.0 / denom
    coef_poi = cross_tp / (denom * length_poi * length_poi)
    local_sens = (coef_tgt * grad_tgt + coef_poi * grad_poi).astype(jnp.bfloat16)
    v_down = lax.all_gather(local_sens[:, 2 * hidden_width :], DP, axis=0, tiled=True)
    full_gu = ag_rows(local_sens[:, : 2 * hidden_width], dp_size)
    v_gate = full_gu[:, :hidden_width]
    v_upper = full_gu[:, hidden_width:]
    tan_gate = matmul(poison_x, v_gate)
    tan_upper = matmul(poison_x, v_upper)
    hidden_tan = (slope_poi * tan_gate * upper_poi + silu_poi * tan_upper).astype(jnp.bfloat16)
    part_tan = matmul(hidden_tan, w_down) + inner_cols(hidden_poi, v_down)
    tan_cols = rs_cols(part_tan.astype(jnp.bfloat16), fs_size)
    back_cols = (tan_cols / poi_total).astype(jnp.bfloat16)
    back_tan = ag_cols(back_cols, fs_size)
    mixed = inner_cols(back_tan, w_down) + matmul(error_poi, v_down)
    gate_total = (
        mixed * upper_poi * slope_poi
        + back_poi * (curve_poi * tan_gate * upper_poi + slope_poi * tan_upper)
    ).astype(jnp.bfloat16)
    upper_total = (mixed * silu_poi + back_poi * slope_poi * tan_gate).astype(jnp.bfloat16)
    gate_dir = (back_poi * slope_poi * upper_poi).astype(jnp.bfloat16)
    upper_dir = (back_poi * silu_poi).astype(jnp.bfloat16)
    part_grad = (
        inner_cols(gate_total, w_gate)
        + inner_cols(upper_total, w_up)
        + inner_cols(gate_dir, v_gate)
        + inner_cols(upper_dir, v_upper)
    )
    grad_cols = rs_cols(part_grad.astype(jnp.bfloat16), fs_size)
    residual_cols = back_cols.astype(jnp.float32)
    scaled = (grad_cols + residual_cols) * float(poi_total * model_width)
    total_sq = psum_all(jnp.sum(scaled * scaled))
    mean_sq = total_sq / float(poi_total * model_width)
    return (scaled * lax.rsqrt(mean_sq + EPSILON), alignment)


def solution(mesh):
    fine = Mesh(mesh.devices.reshape(4, 2, 2, 4, 2), FS + DP)
    in_specs = (
        P(DP, None),
        P(DP, None),
        P(DP, None),
        P(DP, None),
        P(None, FS),
        P(None, FS),
        P(FS, None),
    )
    out_specs = (P(DP, FS), P())
    return jax.shard_map(local, mesh=fine, in_specs=in_specs, out_specs=out_specs, check_vma=False)
```

```python
import jax
import jax.numpy as jnp
from jax import lax
from jax.sharding import Mesh, PartitionSpec as P

EPSILON = 1e-06
FS = ("z", "ylo", "core")
DP = ("x", "yhi")


def rs_cols(part, n):
    rows, cols = part.shape
    r = part.reshape(rows, n, cols // n).transpose(1, 0, 2)
    r = lax.all_to_all(r, FS, 0, 0, tiled=False)
    return jnp.sum(r.astype(jnp.float32), 0)


def ag_cols(piece, n):
    rows, cols = piece.shape
    g = lax.all_to_all(jnp.broadcast_to(piece[None], (n, rows, cols)), FS, 0, 0, tiled=False)
    return g.transpose(1, 0, 2).reshape(rows, n * cols)


def ag_rows(piece, n):
    rows, cols = piece.shape
    g = lax.all_to_all(jnp.broadcast_to(piece[None], (n, rows, cols)), DP, 0, 0, tiled=False)
    return g.reshape(n * rows, cols)


def psum_all(x):
    for axis in ("core", "ylo", "z", "x", "yhi"):
        x = lax.psum(x, axis)
    return x


def silu_parts(preact):
    sigma = jax.nn.sigmoid(preact)
    silu_val = preact * sigma
    slope = sigma * (1.0 + preact * (1.0 - sigma))
    curve = sigma * (1.0 - sigma) * (2.0 + preact * (1.0 - 2.0 * sigma))
    return (silu_val, slope, curve)


def matmul(left, right):
    return jnp.dot(left, right, preferred_element_type=jnp.float32)


def inner_rows(left, right):
    return lax.dot_general(
        left, right, (((0,), (0,)), ((), ())), preferred_element_type=jnp.float32
    )


def inner_cols(left, right):
    return lax.dot_general(
        left, right, (((1,), (1,)), ((), ())), preferred_element_type=jnp.float32
    )


def mlp_forward(inputs, w_gate, w_up, w_down):
    gate_pre = matmul(inputs, w_gate)
    upper = matmul(inputs, w_up)
    silu_val, slope, curve = silu_parts(gate_pre)
    hidden = (silu_val * upper).astype(jnp.bfloat16)
    return (upper, silu_val, slope, curve, hidden, matmul(hidden, w_down))


def backward(inputs, labels, output, upper, silu_val, slope, w_down, token_total):
    error = (
        (inputs.astype(jnp.float32) + output - labels.astype(jnp.float32)) / token_total
    ).astype(jnp.bfloat16)
    back_hidden = inner_cols(error, w_down)
    gate_back = (back_hidden * upper * slope).astype(jnp.bfloat16)
    upper_back = (back_hidden * silu_val).astype(jnp.bfloat16)
    return (error, back_hidden, gate_back, upper_back)


def backward2(error, upper, silu_val, slope, w_down):
    back_hidden = inner_cols(error, w_down)
    gate_back = (back_hidden * upper * slope).astype(jnp.bfloat16)
    upper_back = (back_hidden * silu_val).astype(jnp.bfloat16)
    return (error, back_hidden, gate_back, upper_back)


def grad_rows(inputs, error, hidden, gate_back, upper_back):
    return jnp.concatenate(
        [inner_rows(inputs, gate_back), inner_rows(inputs, upper_back), inner_rows(error, hidden)],
        axis=1,
    )


def local(target_x, target_y, poison_x, poison_y, w_gate, w_up, w_down):
    hidden_width = w_gate.shape[1]
    model_width = w_gate.shape[0]
    dp_size = lax.axis_size(DP)
    fs_size = lax.axis_size(FS)
    tgt_total = target_x.shape[0] * dp_size
    poi_total = poison_x.shape[0] * dp_size
    upper_tgt, silu_tgt, slope_tgt, curve_tgt, hidden_tgt, part_tgt = mlp_forward(
        target_x, w_gate, w_up, w_down
    )
    upper_poi, silu_poi, slope_poi, curve_poi, hidden_poi, part_poi = mlp_forward(
        poison_x, w_gate, w_up, w_down
    )
    n_tgt = target_x.shape[0]
    fidx = lax.axis_index(FS)
    width = model_width // fs_size
    out_cols = rs_cols(
        jnp.concatenate([part_tgt, part_poi], axis=0).astype(jnp.bfloat16), fs_size
    )
    x_cols = lax.dynamic_slice_in_dim(jnp.concatenate([target_x, poison_x], 0), fidx * width, width, 1)
    y_cols = lax.dynamic_slice_in_dim(jnp.concatenate([target_y, poison_y], 0), fidx * width, width, 1)
    scale_rows = jnp.concatenate(
        [jnp.full((n_tgt, 1), float(tgt_total), jnp.float32),
         jnp.full((poison_x.shape[0], 1), float(poi_total), jnp.float32)], 0)
    err_cols = (
        (x_cols.astype(jnp.float32) + out_cols - y_cols.astype(jnp.float32)) / scale_rows
    ).astype(jnp.bfloat16)
    error_all = ag_cols(err_cols, fs_size)
    error_tgt, back_tgt, gback_tgt, uback_tgt = backward2(
        error_all[:n_tgt], upper_tgt, silu_tgt, slope_tgt, w_down
    )
    error_poi, back_poi, gback_poi, uback_poi = backward2(
        error_all[n_tgt:], upper_poi, silu_poi, slope_poi, w_down
    )
    n_poi = poison_x.shape[0]
    rows_d = model_width // dp_size
    x_loc = jnp.concatenate([target_x, poison_x], 0)
    x_rows = lax.all_to_all(
        x_loc.reshape(-1, dp_size, rows_d).transpose(1, 0, 2), DP, 0, 0, tiled=False
    )
    e_rows = lax.all_to_all(
        error_all.reshape(-1, dp_size, rows_d).transpose(1, 0, 2), DP, 0, 0, tiled=False
    )
    factors = jnp.concatenate(
        [
            jnp.concatenate([gback_tgt, uback_tgt, hidden_tgt], 1),
            jnp.concatenate([gback_poi, uback_poi, hidden_poi], 1),
        ],
        0,
    )
    f_all = lax.all_gather(factors, DP, axis=0, tiled=False)
    two = 2 * hidden_width

    def block_grad(xr, er, fa):
        dims = (((0, 1), (0, 1)), ((), ()))
        gu = lax.dot_general(xr, fa[:, :, :two], dims, preferred_element_type=jnp.float32)
        dn = lax.dot_general(er, fa[:, :, two:], dims, preferred_element_type=jnp.float32)
        return jnp.concatenate([gu, dn], 1)

    grad_tgt = block_grad(x_rows[:, :n_tgt], e_rows[:, :n_tgt], f_all[:, :n_tgt])
    grad_poi = block_grad(x_rows[:, n_tgt:], e_rows[:, n_tgt:], f_all[:, n_tgt:])
    norm_tt, norm_pp, cross_tp = psum_all(
        (jnp.sum(grad_tgt * grad_tgt), jnp.sum(grad_poi * grad_poi), jnp.sum(grad_tgt * grad_poi))
    )
    length_tgt = jnp.sqrt(norm_tt + EPSILON)
    length_poi = jnp.sqrt(norm_pp + EPSILON)
    denom = length_tgt * length_poi
    alignment = 1.0 - cross_tp / denom
    coef_tgt = -1.0 / denom
    coef_poi = cross_tp / (denom * length_poi * length_poi)
    local_sens = (coef_tgt * grad_tgt + coef_poi * grad_poi).astype(jnp.bfloat16)
    v_down = lax.all_gather(local_sens[:, 2 * hidden_width :], DP, axis=0, tiled=True)
    full_gu = ag_rows(local_sens[:, : 2 * hidden_width], dp_size)
    v_gate = full_gu[:, :hidden_width]
    v_upper = full_gu[:, hidden_width:]
    tan_gate = matmul(poison_x, v_gate)
    tan_upper = matmul(poison_x, v_upper)
    hidden_tan = (slope_poi * tan_gate * upper_poi + silu_poi * tan_upper).astype(jnp.bfloat16)
    part_tan = matmul(hidden_tan, w_down) + inner_cols(hidden_poi, v_down)
    tan_cols = rs_cols(part_tan.astype(jnp.bfloat16), fs_size)
    back_cols = (tan_cols / poi_total).astype(jnp.bfloat16)
    back_tan = ag_cols(back_cols, fs_size)
    mixed = inner_cols(back_tan, w_down) + matmul(error_poi, v_down)
    gate_total = (
        mixed * upper_poi * slope_poi
        + back_poi * (curve_poi * tan_gate * upper_poi + slope_poi * tan_upper)
    ).astype(jnp.bfloat16)
    upper_total = (mixed * silu_poi + back_poi * slope_poi * tan_gate).astype(jnp.bfloat16)
    gate_dir = (back_poi * slope_poi * upper_poi).astype(jnp.bfloat16)
    upper_dir = (back_poi * silu_poi).astype(jnp.bfloat16)
    part_grad = (
        inner_cols(gate_total, w_gate)
        + inner_cols(upper_total, w_up)
        + inner_cols(gate_dir, v_gate)
        + inner_cols(upper_dir, v_upper)
    )
    grad_cols = rs_cols(part_grad.astype(jnp.bfloat16), fs_size)
    residual_cols = back_cols.astype(jnp.float32)
    scaled = (grad_cols + residual_cols) * float(poi_total * model_width)
    total_sq = psum_all(jnp.sum(scaled * scaled))
    mean_sq = total_sq / float(poi_total * model_width)
    return (scaled * lax.rsqrt(mean_sq + EPSILON), alignment)


def solution(mesh):
    fine = Mesh(mesh.devices.reshape(4, 2, 2, 4, 2), FS + DP)
    in_specs = (
        P(DP, None),
        P(DP, None),
        P(DP, None),
        P(DP, None),
        P(None, FS),
        P(None, FS),
        P(FS, None),
    )
    out_specs = (P(DP, FS), P())
    return jax.shard_map(local, mesh=fine, in_specs=in_specs, out_specs=out_specs, check_vma=False)
```

```python
import jax
import jax.numpy as jnp
from jax import lax
from jax.sharding import Mesh, PartitionSpec as P

EPSILON = 1e-06
FS = ("z", "ylo", "core")
DP = ("x", "yhi")


def rs_cols(part, n):
    rows, cols = part.shape
    r = part.reshape(rows, n, cols // n).transpose(1, 0, 2)
    r = lax.all_to_all(r, FS, 0, 0, tiled=False)
    return jnp.sum(r.astype(jnp.float32), 0)


def ag_cols(piece, n):
    rows, cols = piece.shape
    g = lax.all_to_all(jnp.broadcast_to(piece[None], (n, rows, cols)), FS, 0, 0, tiled=False)
    return g.transpose(1, 0, 2).reshape(rows, n * cols)


def ag_rows(piece, n):
    rows, cols = piece.shape
    g = lax.all_to_all(jnp.broadcast_to(piece[None], (n, rows, cols)), DP, 0, 0, tiled=False)
    return g.reshape(n * rows, cols)


def psum_all(x):
    for axis in ("core", "ylo", "z", "x", "yhi"):
        x = lax.psum(x, axis)
    return x


def silu_parts(preact):
    sigma = jax.nn.sigmoid(preact)
    silu_val = preact * sigma
    slope = sigma * (1.0 + preact * (1.0 - sigma))
    curve = sigma * (1.0 - sigma) * (2.0 + preact * (1.0 - 2.0 * sigma))
    return (silu_val, slope, curve)


def matmul(left, right):
    return jnp.dot(left, right, preferred_element_type=jnp.float32)


def inner_rows(left, right):
    return lax.dot_general(
        left, right, (((0,), (0,)), ((), ())), preferred_element_type=jnp.float32
    )


def inner_cols(left, right):
    return lax.dot_general(
        left, right, (((1,), (1,)), ((), ())), preferred_element_type=jnp.float32
    )


def mlp_forward(inputs, w_gate, w_up, w_down):
    gate_pre = matmul(inputs, w_gate)
    upper = matmul(inputs, w_up)
    silu_val, slope, curve = silu_parts(gate_pre)
    hidden = (silu_val * upper).astype(jnp.bfloat16)
    return (upper, silu_val, slope, curve, hidden, matmul(hidden, w_down))


def backward(inputs, labels, output, upper, silu_val, slope, w_down, token_total):
    error = (
        (inputs.astype(jnp.float32) + output - labels.astype(jnp.float32)) / token_total
    ).astype(jnp.bfloat16)
    back_hidden = inner_cols(error, w_down)
    gate_back = (back_hidden * upper * slope).astype(jnp.bfloat16)
    upper_back = (back_hidden * silu_val).astype(jnp.bfloat16)
    return (error, back_hidden, gate_back, upper_back)


def backward2(error, upper, silu_val, slope, w_down):
    back_hidden = inner_cols(error, w_down)
    gate_back = (back_hidden * upper * slope).astype(jnp.bfloat16)
    upper_back = (back_hidden * silu_val).astype(jnp.bfloat16)
    return (error, back_hidden, gate_back, upper_back)


def grad_rows(inputs, error, hidden, gate_back, upper_back):
    return jnp.concatenate(
        [inner_rows(inputs, gate_back), inner_rows(inputs, upper_back), inner_rows(error, hidden)],
        axis=1,
    )


def local(target_x, target_y, poison_x, poison_y, w_gate, w_up, w_down):
    hidden_width = w_gate.shape[1]
    model_width = w_gate.shape[0]
    dp_size = lax.axis_size(DP)
    fs_size = lax.axis_size(FS)
    tgt_total = target_x.shape[0] * dp_size
    poi_total = poison_x.shape[0] * dp_size
    upper_tgt, silu_tgt, slope_tgt, curve_tgt, hidden_tgt, part_tgt = mlp_forward(
        target_x, w_gate, w_up, w_down
    )
    upper_poi, silu_poi, slope_poi, curve_poi, hidden_poi, part_poi = mlp_forward(
        poison_x, w_gate, w_up, w_down
    )
    n_tgt = target_x.shape[0]
    fidx = lax.axis_index(FS)
    width = model_width // fs_size
    out_cols = rs_cols(
        jnp.concatenate([part_tgt, part_poi], axis=0).astype(jnp.bfloat16), fs_size
    )
    x_loc = jnp.concatenate([target_x, poison_x], 0)
    x_rows = lax.all_to_all(
        x_loc.reshape(-1, dp_size, model_width // dp_size).transpose(1, 0, 2), DP, 0, 0, tiled=False
    )
    x_rows, out_cols = lax.optimization_barrier((x_rows, out_cols))
    x_cols = lax.dynamic_slice_in_dim(jnp.concatenate([target_x, poison_x], 0), fidx * width, width, 1)
    y_cols = lax.dynamic_slice_in_dim(jnp.concatenate([target_y, poison_y], 0), fidx * width, width, 1)
    scale_rows = jnp.concatenate(
        [jnp.full((n_tgt, 1), float(tgt_total), jnp.float32),
         jnp.full((poison_x.shape[0], 1), float(poi_total), jnp.float32)], 0)
    err_cols = (
        (x_cols.astype(jnp.float32) + out_cols - y_cols.astype(jnp.float32)) / scale_rows
    ).astype(jnp.bfloat16)
    error_all = ag_cols(err_cols, fs_size)
    error_tgt, back_tgt, gback_tgt, uback_tgt = backward2(
        error_all[:n_tgt], upper_tgt, silu_tgt, slope_tgt, w_down
    )
    error_poi, back_poi, gback_poi, uback_poi = backward2(
        error_all[n_tgt:], upper_poi, silu_poi, slope_poi, w_down
    )
    n_poi = poison_x.shape[0]
    rows_d = model_width // dp_size
    e_rows = lax.all_to_all(
        error_all.reshape(-1, dp_size, rows_d).transpose(1, 0, 2), DP, 0, 0, tiled=False
    )
    h_all = lax.all_gather(jnp.concatenate([hidden_tgt, hidden_poi], 0), DP, axis=0, tiled=False)
    gu_loc = jnp.concatenate(
        [
            jnp.concatenate([gback_tgt, uback_tgt], 1),
            jnp.concatenate([gback_poi, uback_poi], 1),
        ],
        0,
    )
    gu_all = lax.all_to_all(
        jnp.broadcast_to(gu_loc[None], (dp_size,) + gu_loc.shape), DP, 0, 0, tiled=False
    )

    def block_grad(xr, er, ga, ha):
        dims = (((0, 1), (0, 1)), ((), ()))
        gu = lax.dot_general(xr, ga, dims, preferred_element_type=jnp.float32)
        dn = lax.dot_general(er, ha, dims, preferred_element_type=jnp.float32)
        return jnp.concatenate([gu, dn], 1)

    grad_tgt = block_grad(x_rows[:, :n_tgt], e_rows[:, :n_tgt], gu_all[:, :n_tgt], h_all[:, :n_tgt])
    grad_poi = block_grad(x_rows[:, n_tgt:], e_rows[:, n_tgt:], gu_all[:, n_tgt:], h_all[:, n_tgt:])
    norm_tt, norm_pp, cross_tp = psum_all(
        (jnp.sum(grad_tgt * grad_tgt), jnp.sum(grad_poi * grad_poi), jnp.sum(grad_tgt * grad_poi))
    )
    length_tgt = jnp.sqrt(norm_tt + EPSILON)
    length_poi = jnp.sqrt(norm_pp + EPSILON)
    denom = length_tgt * length_poi
    alignment = 1.0 - cross_tp / denom
    coef_tgt = -1.0 / denom
    coef_poi = cross_tp / (denom * length_poi * length_poi)
    local_sens = (coef_tgt * grad_tgt + coef_poi * grad_poi).astype(jnp.bfloat16)
    v_down = lax.all_gather(local_sens[:, 2 * hidden_width :], DP, axis=0, tiled=True)
    full_gu = ag_rows(local_sens[:, : 2 * hidden_width], dp_size)
    v_gate = full_gu[:, :hidden_width]
    v_upper = full_gu[:, hidden_width:]
    tan_gate = matmul(poison_x, v_gate)
    tan_upper = matmul(poison_x, v_upper)
    hidden_tan = (slope_poi * tan_gate * upper_poi + silu_poi * tan_upper).astype(jnp.bfloat16)
    part_tan = matmul(hidden_tan, w_down) + inner_cols(hidden_poi, v_down)
    tan_cols = rs_cols(part_tan.astype(jnp.bfloat16), fs_size)
    back_cols = (tan_cols / poi_total).astype(jnp.bfloat16)
    back_tan = ag_cols(back_cols, fs_size)
    mixed = inner_cols(back_tan, w_down) + matmul(error_poi, v_down)
    gate_total = (
        mixed * upper_poi * slope_poi
        + back_poi * (curve_poi * tan_gate * upper_poi + slope_poi * tan_upper)
    ).astype(jnp.bfloat16)
    upper_total = (mixed * silu_poi + back_poi * slope_poi * tan_gate).astype(jnp.bfloat16)
    gate_dir = (back_poi * slope_poi * upper_poi).astype(jnp.bfloat16)
    upper_dir = (back_poi * silu_poi).astype(jnp.bfloat16)
    part_grad = (
        inner_cols(gate_total, w_gate)
        + inner_cols(upper_total, w_up)
        + inner_cols(gate_dir, v_gate)
        + inner_cols(upper_dir, v_upper)
    )
    grad_cols = rs_cols(part_grad.astype(jnp.bfloat16), fs_size)
    residual_cols = back_cols.astype(jnp.float32)
    scaled = (grad_cols + residual_cols) * float(poi_total * model_width)
    total_sq = psum_all(jnp.sum(scaled * scaled))
    mean_sq = total_sq / float(poi_total * model_width)
    return (scaled * lax.rsqrt(mean_sq + EPSILON), alignment)


def solution(mesh):
    fine = Mesh(mesh.devices.reshape(4, 2, 2, 4, 2), FS + DP)
    in_specs = (
        P(DP, None),
        P(DP, None),
        P(DP, None),
        P(DP, None),
        P(None, FS),
        P(None, FS),
        P(FS, None),
    )
    out_specs = (P(DP, FS), P())
    return jax.shard_map(local, mesh=fine, in_specs=in_specs, out_specs=out_specs, check_vma=False)
```

```python
import jax
import jax.numpy as jnp
from jax import lax
from jax.sharding import Mesh, PartitionSpec as P

EPSILON = 1e-06
FS = ("z", "ylo", "core")
DP = ("x", "yhi")


def rs_cols(part, n):
    rows, cols = part.shape
    r = part.reshape(rows, n, cols // n).transpose(1, 0, 2)
    r = lax.all_to_all(r, FS, 0, 0, tiled=False)
    return jnp.sum(r.astype(jnp.float32), 0)


def ag_cols(piece, n):
    rows, cols = piece.shape
    g = lax.all_to_all(jnp.broadcast_to(piece[None], (n, rows, cols)), FS, 0, 0, tiled=False)
    return g.transpose(1, 0, 2).reshape(rows, n * cols)


def ag_rows(piece, n):
    rows, cols = piece.shape
    g = lax.all_to_all(jnp.broadcast_to(piece[None], (n, rows, cols)), DP, 0, 0, tiled=False)
    return g.reshape(n * rows, cols)


def exchange_rows(local_x, n):
    pieces = local_x.reshape(local_x.shape[0], n, -1).transpose(1, 0, 2)
    d = lax.axis_index(DP)
    got = [lax.dynamic_index_in_dim(pieces, d, 0, keepdims=False)]
    for s in range(1, n):
        send = lax.dynamic_index_in_dim(pieces, (d + s) % n, 0, keepdims=False)
        got.append(lax.ppermute(send, DP, [(i, (i + s) % n) for i in range(n)]))
    got = jnp.stack(got)
    return jnp.take(got, (d - jnp.arange(n)) % n, axis=0)


def psum_all(x):
    for axis in ("core", "ylo", "z", "x", "yhi"):
        x = lax.psum(x, axis)
    return x


def silu_parts(preact):
    sigma = jax.nn.sigmoid(preact)
    silu_val = preact * sigma
    slope = sigma * (1.0 + preact * (1.0 - sigma))
    curve = sigma * (1.0 - sigma) * (2.0 + preact * (1.0 - 2.0 * sigma))
    return (silu_val, slope, curve)


def matmul(left, right):
    return jnp.dot(left, right, preferred_element_type=jnp.float32)


def inner_rows(left, right):
    return lax.dot_general(
        left, right, (((0,), (0,)), ((), ())), preferred_element_type=jnp.float32
    )


def inner_cols(left, right):
    return lax.dot_general(
        left, right, (((1,), (1,)), ((), ())), preferred_element_type=jnp.float32
    )


def mlp_forward(inputs, w_gate, w_up, w_down):
    gate_pre = matmul(inputs, w_gate)
    upper = matmul(inputs, w_up)
    silu_val, slope, curve = silu_parts(gate_pre)
    hidden = (silu_val * upper).astype(jnp.bfloat16)
    return (upper, silu_val, slope, curve, hidden, matmul(hidden, w_down))


def backward(inputs, labels, output, upper, silu_val, slope, w_down, token_total):
    error = (
        (inputs.astype(jnp.float32) + output - labels.astype(jnp.float32)) / token_total
    ).astype(jnp.bfloat16)
    back_hidden = inner_cols(error, w_down)
    gate_back = (back_hidden * upper * slope).astype(jnp.bfloat16)
    upper_back = (back_hidden * silu_val).astype(jnp.bfloat16)
    return (error, back_hidden, gate_back, upper_back)


def backward2(error, upper, silu_val, slope, w_down):
    back_hidden = inner_cols(error, w_down)
    gate_back = (back_hidden * upper * slope).astype(jnp.bfloat16)
    upper_back = (back_hidden * silu_val).astype(jnp.bfloat16)
    return (error, back_hidden, gate_back, upper_back)


def grad_rows(inputs, error, hidden, gate_back, upper_back):
    return jnp.concatenate(
        [inner_rows(inputs, gate_back), inner_rows(inputs, upper_back), inner_rows(error, hidden)],
        axis=1,
    )


def local(target_x, target_y, poison_x, poison_y, w_gate, w_up, w_down):
    hidden_width = w_gate.shape[1]
    model_width = w_gate.shape[0]
    dp_size = lax.axis_size(DP)
    fs_size = lax.axis_size(FS)
    tgt_total = target_x.shape[0] * dp_size
    poi_total = poison_x.shape[0] * dp_size
    upper_tgt, silu_tgt, slope_tgt, curve_tgt, hidden_tgt, part_tgt = mlp_forward(
        target_x, w_gate, w_up, w_down
    )
    upper_poi, silu_poi, slope_poi, curve_poi, hidden_poi, part_poi = mlp_forward(
        poison_x, w_gate, w_up, w_down
    )
    n_tgt = target_x.shape[0]
    fidx = lax.axis_index(FS)
    width = model_width // fs_size
    out_cols = rs_cols(
        jnp.concatenate([part_tgt, part_poi], axis=0).astype(jnp.bfloat16), fs_size
    )
    x_rows = exchange_rows(jnp.concatenate([target_x, poison_x], 0), dp_size)
    x_rows, out_cols = lax.optimization_barrier((x_rows, out_cols))
    x_cols = lax.dynamic_slice_in_dim(jnp.concatenate([target_x, poison_x], 0), fidx * width, width, 1)
    y_cols = lax.dynamic_slice_in_dim(jnp.concatenate([target_y, poison_y], 0), fidx * width, width, 1)
    scale_rows = jnp.concatenate(
        [jnp.full((n_tgt, 1), float(tgt_total), jnp.float32),
         jnp.full((poison_x.shape[0], 1), float(poi_total), jnp.float32)], 0)
    err_cols = (
        (x_cols.astype(jnp.float32) + out_cols - y_cols.astype(jnp.float32)) / scale_rows
    ).astype(jnp.bfloat16)
    error_all = ag_cols(err_cols, fs_size)
    error_tgt, back_tgt, gback_tgt, uback_tgt = backward2(
        error_all[:n_tgt], upper_tgt, silu_tgt, slope_tgt, w_down
    )
    error_poi, back_poi, gback_poi, uback_poi = backward2(
        error_all[n_tgt:], upper_poi, silu_poi, slope_poi, w_down
    )
    n_poi = poison_x.shape[0]
    rows_d = model_width // dp_size
    e_rows = lax.all_to_all(
        error_all.reshape(-1, dp_size, rows_d).transpose(1, 0, 2), DP, 0, 0, tiled=False
    )
    h_all = lax.all_gather(jnp.concatenate([hidden_tgt, hidden_poi], 0), DP, axis=0, tiled=False)
    gu_loc = jnp.concatenate(
        [
            jnp.concatenate([gback_tgt, uback_tgt], 1),
            jnp.concatenate([gback_poi, uback_poi], 1),
        ],
        0,
    )
    gu_all = lax.all_to_all(
        jnp.broadcast_to(gu_loc[None], (dp_size,) + gu_loc.shape), DP, 0, 0, tiled=False
    )

    def block_grad(xr, er, ga, ha):
        dims = (((0, 1), (0, 1)), ((), ()))
        gu = lax.dot_general(xr, ga, dims, preferred_element_type=jnp.float32)
        dn = lax.dot_general(er, ha, dims, preferred_element_type=jnp.float32)
        return jnp.concatenate([gu, dn], 1)

    grad_tgt = block_grad(x_rows[:, :n_tgt], e_rows[:, :n_tgt], gu_all[:, :n_tgt], h_all[:, :n_tgt])
    grad_poi = block_grad(x_rows[:, n_tgt:], e_rows[:, n_tgt:], gu_all[:, n_tgt:], h_all[:, n_tgt:])
    norm_tt, norm_pp, cross_tp = psum_all(
        (jnp.sum(grad_tgt * grad_tgt), jnp.sum(grad_poi * grad_poi), jnp.sum(grad_tgt * grad_poi))
    )
    length_tgt = jnp.sqrt(norm_tt + EPSILON)
    length_poi = jnp.sqrt(norm_pp + EPSILON)
    denom = length_tgt * length_poi
    alignment = 1.0 - cross_tp / denom
    coef_tgt = -1.0 / denom
    coef_poi = cross_tp / (denom * length_poi * length_poi)
    local_sens = (coef_tgt * grad_tgt + coef_poi * grad_poi).astype(jnp.bfloat16)
    v_down = lax.all_gather(local_sens[:, 2 * hidden_width :], DP, axis=0, tiled=True)
    full_gu = ag_rows(local_sens[:, : 2 * hidden_width], dp_size)
    v_gate = full_gu[:, :hidden_width]
    v_upper = full_gu[:, hidden_width:]
    tan_gate = matmul(poison_x, v_gate)
    tan_upper = matmul(poison_x, v_upper)
    hidden_tan = (slope_poi * tan_gate * upper_poi + silu_poi * tan_upper).astype(jnp.bfloat16)
    part_tan = matmul(hidden_tan, w_down) + inner_cols(hidden_poi, v_down)
    tan_cols = rs_cols(part_tan.astype(jnp.bfloat16), fs_size)
    back_cols = (tan_cols / poi_total).astype(jnp.bfloat16)
    back_tan = ag_cols(back_cols, fs_size)
    mixed = inner_cols(back_tan, w_down) + matmul(error_poi, v_down)
    gate_total = (
        mixed * upper_poi * slope_poi
        + back_poi * (curve_poi * tan_gate * upper_poi + slope_poi * tan_upper)
    ).astype(jnp.bfloat16)
    upper_total = (mixed * silu_poi + back_poi * slope_poi * tan_gate).astype(jnp.bfloat16)
    gate_dir = (back_poi * slope_poi * upper_poi).astype(jnp.bfloat16)
    upper_dir = (back_poi * silu_poi).astype(jnp.bfloat16)
    part_grad = (
        inner_cols(gate_total, w_gate)
        + inner_cols(upper_total, w_up)
        + inner_cols(gate_dir, v_gate)
        + inner_cols(upper_dir, v_upper)
    )
    grad_cols = rs_cols(part_grad.astype(jnp.bfloat16), fs_size)
    residual_cols = back_cols.astype(jnp.float32)
    scaled = (grad_cols + residual_cols) * float(poi_total * model_width)
    total_sq = psum_all(jnp.sum(scaled * scaled))
    mean_sq = total_sq / float(poi_total * model_width)
    return (scaled * lax.rsqrt(mean_sq + EPSILON), alignment)


def solution(mesh):
    fine = Mesh(mesh.devices.reshape(4, 2, 2, 4, 2), FS + DP)
    in_specs = (
        P(DP, None),
        P(DP, None),
        P(DP, None),
        P(DP, None),
        P(None, FS),
        P(None, FS),
        P(FS, None),
    )
    out_specs = (P(DP, FS), P())
    return jax.shard_map(local, mesh=fine, in_specs=in_specs, out_specs=out_specs, check_vma=False)
```

```python
import jax
import jax.numpy as jnp
from jax import lax
from jax.sharding import Mesh, PartitionSpec as P

EPSILON = 1e-06
FS = ("z", "ylo", "core")
DP = ("x", "yhi")


def rs_cols(part, n):
    rows, cols = part.shape
    r = part.reshape(rows, n, cols // n).transpose(1, 0, 2)
    r = lax.all_to_all(r, FS, 0, 0, tiled=False)
    return jnp.sum(r.astype(jnp.float32), 0)


def ag_cols(piece, n):
    rows, cols = piece.shape
    g = lax.all_to_all(jnp.broadcast_to(piece[None], (n, rows, cols)), FS, 0, 0, tiled=False)
    return g.transpose(1, 0, 2).reshape(rows, n * cols)


def ag_rows(piece, n):
    rows, cols = piece.shape
    g = lax.all_to_all(jnp.broadcast_to(piece[None], (n, rows, cols)), DP, 0, 0, tiled=False)
    return g.reshape(n * rows, cols)


def psum_all(x):
    for axis in ("core", "ylo", "z", "x", "yhi"):
        x = lax.psum(x, axis)
    return x


def silu_parts(preact):
    sigma = jax.nn.sigmoid(preact)
    silu_val = preact * sigma
    slope = sigma * (1.0 + preact * (1.0 - sigma))
    curve = sigma * (1.0 - sigma) * (2.0 + preact * (1.0 - 2.0 * sigma))
    return (silu_val, slope, curve)


def matmul(left, right):
    return jnp.dot(left, right, preferred_element_type=jnp.float32)


def inner_rows(left, right):
    return lax.dot_general(
        left, right, (((0,), (0,)), ((), ())), preferred_element_type=jnp.float32
    )


def inner_cols(left, right):
    return lax.dot_general(
        left, right, (((1,), (1,)), ((), ())), preferred_element_type=jnp.float32
    )


def mlp_forward(inputs, w_gate, w_up, w_down):
    gate_pre = matmul(inputs, w_gate)
    upper = matmul(inputs, w_up)
    silu_val, slope, curve = silu_parts(gate_pre)
    hidden = (silu_val * upper).astype(jnp.bfloat16)
    return (upper, silu_val, slope, curve, hidden, matmul(hidden, w_down))


def backward(inputs, labels, output, upper, silu_val, slope, w_down, token_total):
    error = (
        (inputs.astype(jnp.float32) + output - labels.astype(jnp.float32)) / token_total
    ).astype(jnp.bfloat16)
    back_hidden = inner_cols(error, w_down)
    gate_back = (back_hidden * upper * slope).astype(jnp.bfloat16)
    upper_back = (back_hidden * silu_val).astype(jnp.bfloat16)
    return (error, back_hidden, gate_back, upper_back)


def backward2(error, upper, silu_val, slope, w_down):
    back_hidden = inner_cols(error, w_down)
    gate_back = (back_hidden * upper * slope).astype(jnp.bfloat16)
    upper_back = (back_hidden * silu_val).astype(jnp.bfloat16)
    return (error, back_hidden, gate_back, upper_back)


def grad_rows(inputs, error, hidden, gate_back, upper_back):
    return jnp.concatenate(
        [inner_rows(inputs, gate_back), inner_rows(inputs, upper_back), inner_rows(error, hidden)],
        axis=1,
    )


def local(target_x, target_y, poison_x, poison_y, w_gate, w_up, w_down):
    hidden_width = w_gate.shape[1]
    model_width = w_gate.shape[0]
    dp_size = lax.axis_size(DP)
    fs_size = lax.axis_size(FS)
    tgt_total = target_x.shape[0] * dp_size
    poi_total = poison_x.shape[0] * dp_size
    upper_tgt, silu_tgt, slope_tgt, curve_tgt, hidden_tgt, part_tgt = mlp_forward(
        target_x, w_gate, w_up, w_down
    )
    upper_poi, silu_poi, slope_poi, curve_poi, hidden_poi, part_poi = mlp_forward(
        poison_x, w_gate, w_up, w_down
    )
    n_tgt = target_x.shape[0]
    fidx = lax.axis_index(FS)
    width = model_width // fs_size
    x_loc = jnp.concatenate([target_x, poison_x], 0)
    x_rows = lax.all_to_all(
        x_loc.reshape(-1, dp_size, model_width // dp_size).transpose(1, 0, 2), DP, 0, 0, tiled=False
    )
    x_rows, part_tgt, part_poi = lax.optimization_barrier((x_rows, part_tgt, part_poi))
    out_cols = rs_cols(
        jnp.concatenate([part_tgt, part_poi], axis=0).astype(jnp.bfloat16), fs_size
    )
    x_cols = lax.dynamic_slice_in_dim(jnp.concatenate([target_x, poison_x], 0), fidx * width, width, 1)
    y_cols = lax.dynamic_slice_in_dim(jnp.concatenate([target_y, poison_y], 0), fidx * width, width, 1)
    scale_rows = jnp.concatenate(
        [jnp.full((n_tgt, 1), float(tgt_total), jnp.float32),
         jnp.full((poison_x.shape[0], 1), float(poi_total), jnp.float32)], 0)
    err_cols = (
        (x_cols.astype(jnp.float32) + out_cols - y_cols.astype(jnp.float32)) / scale_rows
    ).astype(jnp.bfloat16)
    error_all = ag_cols(err_cols, fs_size)
    error_tgt, back_tgt, gback_tgt, uback_tgt = backward2(
        error_all[:n_tgt], upper_tgt, silu_tgt, slope_tgt, w_down
    )
    error_poi, back_poi, gback_poi, uback_poi = backward2(
        error_all[n_tgt:], upper_poi, silu_poi, slope_poi, w_down
    )
    n_poi = poison_x.shape[0]
    rows_d = model_width // dp_size
    e_rows = lax.all_to_all(
        error_all.reshape(-1, dp_size, rows_d).transpose(1, 0, 2), DP, 0, 0, tiled=False
    )
    h_all = lax.all_gather(jnp.concatenate([hidden_tgt, hidden_poi], 0), DP, axis=0, tiled=False)
    gu_loc = jnp.concatenate(
        [
            jnp.concatenate([gback_tgt, uback_tgt], 1),
            jnp.concatenate([gback_poi, uback_poi], 1),
        ],
        0,
    )
    gu_all = lax.all_to_all(
        jnp.broadcast_to(gu_loc[None], (dp_size,) + gu_loc.shape), DP, 0, 0, tiled=False
    )

    def block_grad(xr, er, ga, ha):
        dims = (((0, 1), (0, 1)), ((), ()))
        gu = lax.dot_general(xr, ga, dims, preferred_element_type=jnp.float32)
        dn = lax.dot_general(er, ha, dims, preferred_element_type=jnp.float32)
        return jnp.concatenate([gu, dn], 1)

    grad_tgt = block_grad(x_rows[:, :n_tgt], e_rows[:, :n_tgt], gu_all[:, :n_tgt], h_all[:, :n_tgt])
    grad_poi = block_grad(x_rows[:, n_tgt:], e_rows[:, n_tgt:], gu_all[:, n_tgt:], h_all[:, n_tgt:])
    norm_tt, norm_pp, cross_tp = psum_all(
        (jnp.sum(grad_tgt * grad_tgt), jnp.sum(grad_poi * grad_poi), jnp.sum(grad_tgt * grad_poi))
    )
    length_tgt = jnp.sqrt(norm_tt + EPSILON)
    length_poi = jnp.sqrt(norm_pp + EPSILON)
    denom = length_tgt * length_poi
    alignment = 1.0 - cross_tp / denom
    coef_tgt = -1.0 / denom
    coef_poi = cross_tp / (denom * length_poi * length_poi)
    local_sens = (coef_tgt * grad_tgt + coef_poi * grad_poi).astype(jnp.bfloat16)
    v_down = lax.all_gather(local_sens[:, 2 * hidden_width :], DP, axis=0, tiled=True)
    full_gu = ag_rows(local_sens[:, : 2 * hidden_width], dp_size)
    v_gate = full_gu[:, :hidden_width]
    v_upper = full_gu[:, hidden_width:]
    tan_gate = matmul(poison_x, v_gate)
    tan_upper = matmul(poison_x, v_upper)
    hidden_tan = (slope_poi * tan_gate * upper_poi + silu_poi * tan_upper).astype(jnp.bfloat16)
    part_tan = matmul(hidden_tan, w_down) + inner_cols(hidden_poi, v_down)
    tan_cols = rs_cols(part_tan.astype(jnp.bfloat16), fs_size)
    back_cols = (tan_cols / poi_total).astype(jnp.bfloat16)
    back_tan = ag_cols(back_cols, fs_size)
    mixed = inner_cols(back_tan, w_down) + matmul(error_poi, v_down)
    gate_total = (
        mixed * upper_poi * slope_poi
        + back_poi * (curve_poi * tan_gate * upper_poi + slope_poi * tan_upper)
    ).astype(jnp.bfloat16)
    upper_total = (mixed * silu_poi + back_poi * slope_poi * tan_gate).astype(jnp.bfloat16)
    gate_dir = (back_poi * slope_poi * upper_poi).astype(jnp.bfloat16)
    upper_dir = (back_poi * silu_poi).astype(jnp.bfloat16)
    part_grad = (
        inner_cols(gate_total, w_gate)
        + inner_cols(upper_total, w_up)
        + inner_cols(gate_dir, v_gate)
        + inner_cols(upper_dir, v_upper)
    )
    grad_cols = rs_cols(part_grad.astype(jnp.bfloat16), fs_size)
    residual_cols = back_cols.astype(jnp.float32)
    scaled = (grad_cols + residual_cols) * float(poi_total * model_width)
    total_sq = psum_all(jnp.sum(scaled * scaled))
    mean_sq = total_sq / float(poi_total * model_width)
    return (scaled * lax.rsqrt(mean_sq + EPSILON), alignment)


def solution(mesh):
    fine = Mesh(mesh.devices.reshape(4, 2, 2, 4, 2), FS + DP)
    in_specs = (
        P(DP, None),
        P(DP, None),
        P(DP, None),
        P(DP, None),
        P(None, FS),
        P(None, FS),
        P(FS, None),
    )
    out_specs = (P(DP, FS), P())
    return jax.shard_map(local, mesh=fine, in_specs=in_specs, out_specs=out_specs, check_vma=False)
```

```python
import jax
import jax.numpy as jnp
from jax import lax
from jax.sharding import Mesh, PartitionSpec as P

EPSILON = 1e-06
FS = ("z", "ylo", "core")
DP = ("x", "yhi")


def rs_cols(part, n):
    rows, cols = part.shape
    r = part.reshape(rows, n, cols // n).transpose(1, 0, 2)
    r = lax.all_to_all(r, FS, 0, 0, tiled=False)
    return jnp.sum(r.astype(jnp.float32), 0)


def ag_cols(piece, n):
    rows, cols = piece.shape
    g = lax.all_to_all(jnp.broadcast_to(piece[None], (n, rows, cols)), FS, 0, 0, tiled=False)
    return g.transpose(1, 0, 2).reshape(rows, n * cols)


def ag_rows(piece, n):
    rows, cols = piece.shape
    g = lax.all_to_all(jnp.broadcast_to(piece[None], (n, rows, cols)), DP, 0, 0, tiled=False)
    return g.reshape(n * rows, cols)


def psum_all(x):
    for axis in ("core", "ylo", "z", "x", "yhi"):
        x = lax.psum(x, axis)
    return x


def silu_parts(preact):
    sigma = jax.nn.sigmoid(preact)
    silu_val = preact * sigma
    slope = sigma * (1.0 + preact * (1.0 - sigma))
    curve = sigma * (1.0 - sigma) * (2.0 + preact * (1.0 - 2.0 * sigma))
    return (silu_val, slope, curve)


def matmul(left, right):
    return jnp.dot(left, right, preferred_element_type=jnp.float32)


def inner_rows(left, right):
    return lax.dot_general(
        left, right, (((0,), (0,)), ((), ())), preferred_element_type=jnp.float32
    )


def inner_cols(left, right):
    return lax.dot_general(
        left, right, (((1,), (1,)), ((), ())), preferred_element_type=jnp.float32
    )


def mlp_forward(inputs, w_gate, w_up, w_down):
    gate_pre = matmul(inputs, w_gate)
    upper = matmul(inputs, w_up)
    silu_val, slope, curve = silu_parts(gate_pre)
    hidden = (silu_val * upper).astype(jnp.bfloat16)
    return (upper, silu_val, slope, curve, hidden, matmul(hidden, w_down))


def backward(inputs, labels, output, upper, silu_val, slope, w_down, token_total):
    error = (
        (inputs.astype(jnp.float32) + output - labels.astype(jnp.float32)) / token_total
    ).astype(jnp.bfloat16)
    back_hidden = inner_cols(error, w_down)
    gate_back = (back_hidden * upper * slope).astype(jnp.bfloat16)
    upper_back = (back_hidden * silu_val).astype(jnp.bfloat16)
    return (error, back_hidden, gate_back, upper_back)


def backward2(error, upper, silu_val, slope, w_down):
    back_hidden = inner_cols(error, w_down)
    gate_back = (back_hidden * upper * slope).astype(jnp.bfloat16)
    upper_back = (back_hidden * silu_val).astype(jnp.bfloat16)
    return (error, back_hidden, gate_back, upper_back)


def grad_rows(inputs, error, hidden, gate_back, upper_back):
    return jnp.concatenate(
        [inner_rows(inputs, gate_back), inner_rows(inputs, upper_back), inner_rows(error, hidden)],
        axis=1,
    )


def local(target_x, target_y, poison_x, poison_y, w_gate, w_up, w_down):
    hidden_width = w_gate.shape[1]
    model_width = w_gate.shape[0]
    dp_size = lax.axis_size(DP)
    fs_size = lax.axis_size(FS)
    tgt_total = target_x.shape[0] * dp_size
    poi_total = poison_x.shape[0] * dp_size
    upper_tgt, silu_tgt, slope_tgt, curve_tgt, hidden_tgt, part_tgt = mlp_forward(
        target_x, w_gate, w_up, w_down
    )
    upper_poi, silu_poi, slope_poi, curve_poi, hidden_poi, part_poi = mlp_forward(
        poison_x, w_gate, w_up, w_down
    )
    n_tgt = target_x.shape[0]
    fidx = lax.axis_index(FS)
    width = model_width // fs_size
    x_loc = jnp.concatenate([target_x, poison_x], 0)
    x_rows = lax.all_to_all(
        x_loc.reshape(-1, dp_size, model_width // dp_size).transpose(1, 0, 2), DP, 0, 0, tiled=False
    )
    x_rows, part_tgt, part_poi = lax.optimization_barrier((x_rows, part_tgt, part_poi))
    out_cols = rs_cols(
        jnp.concatenate([part_tgt, part_poi], axis=0).astype(jnp.bfloat16), fs_size
    )
    x_cols = lax.dynamic_slice_in_dim(jnp.concatenate([target_x, poison_x], 0), fidx * width, width, 1)
    y_cols = lax.dynamic_slice_in_dim(jnp.concatenate([target_y, poison_y], 0), fidx * width, width, 1)
    scale_rows = jnp.concatenate(
        [jnp.full((n_tgt, 1), float(tgt_total), jnp.float32),
         jnp.full((poison_x.shape[0], 1), float(poi_total), jnp.float32)], 0)
    err_cols = (
        (x_cols.astype(jnp.float32) + out_cols - y_cols.astype(jnp.float32)) / scale_rows
    ).astype(jnp.bfloat16)
    error_all = ag_cols(err_cols, fs_size)
    error_tgt, back_tgt, gback_tgt, uback_tgt = backward2(
        error_all[:n_tgt], upper_tgt, silu_tgt, slope_tgt, w_down
    )
    error_poi, back_poi, gback_poi, uback_poi = backward2(
        error_all[n_tgt:], upper_poi, silu_poi, slope_poi, w_down
    )
    n_poi = poison_x.shape[0]
    rows_d = model_width // dp_size
    joint_dn = lax.psum_scatter(
        jnp.concatenate(
            [inner_rows(error_tgt, hidden_tgt), inner_rows(error_poi, hidden_poi)], axis=1
        ).astype(jnp.bfloat16),
        DP,
        scatter_dimension=0,
        tiled=True,
    ).astype(jnp.float32)
    gu_loc = jnp.concatenate(
        [
            jnp.concatenate([gback_tgt, uback_tgt], 1),
            jnp.concatenate([gback_poi, uback_poi], 1),
        ],
        0,
    )
    gu_all = lax.all_to_all(
        jnp.broadcast_to(gu_loc[None], (dp_size,) + gu_loc.shape), DP, 0, 0, tiled=False
    )
    dims = (((0, 1), (0, 1)), ((), ()))
    gu_tgt_blk = lax.dot_general(
        x_rows[:, :n_tgt], gu_all[:, :n_tgt], dims, preferred_element_type=jnp.float32
    )
    gu_poi_blk = lax.dot_general(
        x_rows[:, n_tgt:], gu_all[:, n_tgt:], dims, preferred_element_type=jnp.float32
    )
    grad_tgt = jnp.concatenate([gu_tgt_blk, joint_dn[:, :hidden_width]], 1)
    grad_poi = jnp.concatenate([gu_poi_blk, joint_dn[:, hidden_width:]], 1)
    norm_tt, norm_pp, cross_tp = psum_all(
        (jnp.sum(grad_tgt * grad_tgt), jnp.sum(grad_poi * grad_poi), jnp.sum(grad_tgt * grad_poi))
    )
    length_tgt = jnp.sqrt(norm_tt + EPSILON)
    length_poi = jnp.sqrt(norm_pp + EPSILON)
    denom = length_tgt * length_poi
    alignment = 1.0 - cross_tp / denom
    coef_tgt = -1.0 / denom
    coef_poi = cross_tp / (denom * length_poi * length_poi)
    local_sens = (coef_tgt * grad_tgt + coef_poi * grad_poi).astype(jnp.bfloat16)
    v_down = lax.all_gather(local_sens[:, 2 * hidden_width :], DP, axis=0, tiled=True)
    full_gu = ag_rows(local_sens[:, : 2 * hidden_width], dp_size)
    v_gate = full_gu[:, :hidden_width]
    v_upper = full_gu[:, hidden_width:]
    tan_gate = matmul(poison_x, v_gate)
    tan_upper = matmul(poison_x, v_upper)
    hidden_tan = (slope_poi * tan_gate * upper_poi + silu_poi * tan_upper).astype(jnp.bfloat16)
    part_tan = matmul(hidden_tan, w_down) + inner_cols(hidden_poi, v_down)
    tan_cols = rs_cols(part_tan.astype(jnp.bfloat16), fs_size)
    back_cols = (tan_cols / poi_total).astype(jnp.bfloat16)
    back_tan = ag_cols(back_cols, fs_size)
    mixed = inner_cols(back_tan, w_down) + matmul(error_poi, v_down)
    gate_total = (
        mixed * upper_poi * slope_poi
        + back_poi * (curve_poi * tan_gate * upper_poi + slope_poi * tan_upper)
    ).astype(jnp.bfloat16)
    upper_total = (mixed * silu_poi + back_poi * slope_poi * tan_gate).astype(jnp.bfloat16)
    gate_dir = (back_poi * slope_poi * upper_poi).astype(jnp.bfloat16)
    upper_dir = (back_poi * silu_poi).astype(jnp.bfloat16)
    part_grad = (
        inner_cols(gate_total, w_gate)
        + inner_cols(upper_total, w_up)
        + inner_cols(gate_dir, v_gate)
        + inner_cols(upper_dir, v_upper)
    )
    grad_cols = rs_cols(part_grad.astype(jnp.bfloat16), fs_size)
    residual_cols = back_cols.astype(jnp.float32)
    scaled = (grad_cols + residual_cols) * float(poi_total * model_width)
    total_sq = psum_all(jnp.sum(scaled * scaled))
    mean_sq = total_sq / float(poi_total * model_width)
    return (scaled * lax.rsqrt(mean_sq + EPSILON), alignment)


def solution(mesh):
    fine = Mesh(mesh.devices.reshape(4, 2, 2, 4, 2), FS + DP)
    in_specs = (
        P(DP, None),
        P(DP, None),
        P(DP, None),
        P(DP, None),
        P(None, FS),
        P(None, FS),
        P(FS, None),
    )
    out_specs = (P(DP, FS), P())
    return jax.shard_map(local, mesh=fine, in_specs=in_specs, out_specs=out_specs, check_vma=False)
```

```python
import jax
import jax.numpy as jnp
from jax import lax
from jax.sharding import Mesh, PartitionSpec as P

EPSILON = 1e-06
FS = ("z", "ylo", "core")
DP = ("x", "yhi")


def rs_cols(part, n):
    rows, cols = part.shape
    r = part.reshape(rows, n, cols // n).transpose(1, 0, 2)
    r = lax.all_to_all(r, FS, 0, 0, tiled=False)
    return jnp.sum(r.astype(jnp.float32), 0)


def ag_cols(piece, n):
    rows, cols = piece.shape
    g = lax.all_to_all(jnp.broadcast_to(piece[None], (n, rows, cols)), FS, 0, 0, tiled=False)
    return g.transpose(1, 0, 2).reshape(rows, n * cols)


def ag_rows(piece, n):
    rows, cols = piece.shape
    g = lax.all_to_all(jnp.broadcast_to(piece[None], (n, rows, cols)), DP, 0, 0, tiled=False)
    return g.reshape(n * rows, cols)


def psum_all(x):
    for axis in ("core", "ylo", "z", "x", "yhi"):
        x = lax.psum(x, axis)
    return x


def silu_parts(preact):
    sigma = jax.nn.sigmoid(preact)
    silu_val = preact * sigma
    slope = sigma * (1.0 + preact * (1.0 - sigma))
    curve = sigma * (1.0 - sigma) * (2.0 + preact * (1.0 - 2.0 * sigma))
    return (silu_val, slope, curve)


def matmul(left, right):
    return jnp.dot(left, right, preferred_element_type=jnp.float32)


def inner_rows(left, right):
    return lax.dot_general(
        left, right, (((0,), (0,)), ((), ())), preferred_element_type=jnp.float32
    )


def inner_cols(left, right):
    return lax.dot_general(
        left, right, (((1,), (1,)), ((), ())), preferred_element_type=jnp.float32
    )


def mlp_forward(inputs, w_gate, w_up, w_down):
    gate_pre = matmul(inputs, w_gate)
    upper = matmul(inputs, w_up)
    silu_val, slope, curve = silu_parts(gate_pre)
    hidden = (silu_val * upper).astype(jnp.bfloat16)
    return (upper, silu_val, slope, curve, hidden, matmul(hidden, w_down))


def backward(inputs, labels, output, upper, silu_val, slope, w_down, token_total):
    error = (
        (inputs.astype(jnp.float32) + output - labels.astype(jnp.float32)) / token_total
    ).astype(jnp.bfloat16)
    back_hidden = inner_cols(error, w_down)
    gate_back = (back_hidden * upper * slope).astype(jnp.bfloat16)
    upper_back = (back_hidden * silu_val).astype(jnp.bfloat16)
    return (error, back_hidden, gate_back, upper_back)


def backward2(error, upper, silu_val, slope, w_down):
    back_hidden = inner_cols(error, w_down)
    gate_back = (back_hidden * upper * slope).astype(jnp.bfloat16)
    upper_back = (back_hidden * silu_val).astype(jnp.bfloat16)
    return (error, back_hidden, gate_back, upper_back)


def grad_rows(inputs, error, hidden, gate_back, upper_back):
    return jnp.concatenate(
        [inner_rows(inputs, gate_back), inner_rows(inputs, upper_back), inner_rows(error, hidden)],
        axis=1,
    )


def local(target_x, target_y, poison_x, poison_y, w_gate, w_up, w_down):
    hidden_width = w_gate.shape[1]
    model_width = w_gate.shape[0]
    dp_size = lax.axis_size(DP)
    fs_size = lax.axis_size(FS)
    tgt_total = target_x.shape[0] * dp_size
    poi_total = poison_x.shape[0] * dp_size
    upper_tgt, silu_tgt, slope_tgt, curve_tgt, hidden_tgt, part_tgt = mlp_forward(
        target_x, w_gate, w_up, w_down
    )
    upper_poi, silu_poi, slope_poi, curve_poi, hidden_poi, part_poi = mlp_forward(
        poison_x, w_gate, w_up, w_down
    )
    n_tgt = target_x.shape[0]
    fidx = lax.axis_index(FS)
    width = model_width // fs_size
    x_loc = jnp.concatenate([target_x, poison_x], 0)
    x_rows = lax.all_to_all(
        x_loc.reshape(-1, dp_size, model_width // dp_size).transpose(1, 0, 2), DP, 0, 0, tiled=False
    )
    x_rows, part_tgt, part_poi = lax.optimization_barrier((x_rows, part_tgt, part_poi))
    out_cols = rs_cols(
        jnp.concatenate([part_tgt, part_poi], axis=0).astype(jnp.bfloat16), fs_size
    )
    x_cols = lax.dynamic_slice_in_dim(jnp.concatenate([target_x, poison_x], 0), fidx * width, width, 1)
    y_cols = lax.dynamic_slice_in_dim(jnp.concatenate([target_y, poison_y], 0), fidx * width, width, 1)
    scale_rows = jnp.concatenate(
        [jnp.full((n_tgt, 1), float(tgt_total), jnp.float32),
         jnp.full((poison_x.shape[0], 1), float(poi_total), jnp.float32)], 0)
    err_cols = (
        (x_cols.astype(jnp.float32) + out_cols - y_cols.astype(jnp.float32)) / scale_rows
    ).astype(jnp.bfloat16)
    error_all = ag_cols(err_cols, fs_size)
    error_tgt, back_tgt, gback_tgt, uback_tgt = backward2(
        error_all[:n_tgt], upper_tgt, silu_tgt, slope_tgt, w_down
    )
    error_poi, back_poi, gback_poi, uback_poi = backward2(
        error_all[n_tgt:], upper_poi, silu_poi, slope_poi, w_down
    )
    n_poi = poison_x.shape[0]
    rows_d = model_width // dp_size
    e_rows = lax.all_to_all(
        error_all.reshape(-1, dp_size, rows_d).transpose(1, 0, 2), DP, 0, 0, tiled=False
    )
    h_all = lax.all_gather(jnp.concatenate([hidden_tgt, hidden_poi], 0), DP, axis=0, tiled=False)
    gu_loc = jnp.concatenate(
        [
            jnp.concatenate([gback_tgt, uback_tgt], 1),
            jnp.concatenate([gback_poi, uback_poi], 1),
        ],
        0,
    )
    gu_all = lax.all_to_all(
        jnp.broadcast_to(gu_loc[None], (dp_size,) + gu_loc.shape), DP, 0, 0, tiled=False
    )

    def block_grad(xr, er, ga, ha):
        dims = (((0, 1), (0, 1)), ((), ()))
        gu = lax.dot_general(xr, ga, dims, preferred_element_type=jnp.float32)
        dn = lax.dot_general(er, ha, dims, preferred_element_type=jnp.float32)
        return jnp.concatenate([gu, dn], 1)

    grad_tgt = block_grad(x_rows[:, :n_tgt], e_rows[:, :n_tgt], gu_all[:, :n_tgt], h_all[:, :n_tgt])
    grad_poi = block_grad(x_rows[:, n_tgt:], e_rows[:, n_tgt:], gu_all[:, n_tgt:], h_all[:, n_tgt:])
    norm_tt, norm_pp, cross_tp = psum_all(
        (jnp.sum(grad_tgt * grad_tgt), jnp.sum(grad_poi * grad_poi), jnp.sum(grad_tgt * grad_poi))
    )
    length_tgt = jnp.sqrt(norm_tt + EPSILON)
    length_poi = jnp.sqrt(norm_pp + EPSILON)
    denom = length_tgt * length_poi
    alignment = 1.0 - cross_tp / denom
    coef_tgt = -1.0 / denom
    coef_poi = cross_tp / (denom * length_poi * length_poi)
    local_sens = (coef_tgt * grad_tgt + coef_poi * grad_poi).astype(jnp.bfloat16)
    cut = hidden_width + hidden_width // 2
    tail = lax.all_gather(local_sens[:, cut:], DP, axis=0, tiled=True)
    head = ag_rows(local_sens[:, :cut], dp_size)
    v_gate = head[:, :hidden_width]
    v_upper = jnp.concatenate([head[:, hidden_width:], tail[:, : cut - hidden_width]], 1)
    v_down = tail[:, cut - hidden_width :]
    tan_gate = matmul(poison_x, v_gate)
    tan_upper = matmul(poison_x, v_upper)
    hidden_tan = (slope_poi * tan_gate * upper_poi + silu_poi * tan_upper).astype(jnp.bfloat16)
    part_tan = matmul(hidden_tan, w_down) + inner_cols(hidden_poi, v_down)
    tan_cols = rs_cols(part_tan.astype(jnp.bfloat16), fs_size)
    back_cols = (tan_cols / poi_total).astype(jnp.bfloat16)
    back_tan = ag_cols(back_cols, fs_size)
    mixed = inner_cols(back_tan, w_down) + matmul(error_poi, v_down)
    gate_total = (
        mixed * upper_poi * slope_poi
        + back_poi * (curve_poi * tan_gate * upper_poi + slope_poi * tan_upper)
    ).astype(jnp.bfloat16)
    upper_total = (mixed * silu_poi + back_poi * slope_poi * tan_gate).astype(jnp.bfloat16)
    gate_dir = (back_poi * slope_poi * upper_poi).astype(jnp.bfloat16)
    upper_dir = (back_poi * silu_poi).astype(jnp.bfloat16)
    part_grad = (
        inner_cols(gate_total, w_gate)
        + inner_cols(upper_total, w_up)
        + inner_cols(gate_dir, v_gate)
        + inner_cols(upper_dir, v_upper)
    )
    grad_cols = rs_cols(part_grad.astype(jnp.bfloat16), fs_size)
    residual_cols = back_cols.astype(jnp.float32)
    scaled = (grad_cols + residual_cols) * float(poi_total * model_width)
    total_sq = psum_all(jnp.sum(scaled * scaled))
    mean_sq = total_sq / float(poi_total * model_width)
    return (scaled * lax.rsqrt(mean_sq + EPSILON), alignment)


def solution(mesh):
    fine = Mesh(mesh.devices.reshape(4, 2, 2, 4, 2), FS + DP)
    in_specs = (
        P(DP, None),
        P(DP, None),
        P(DP, None),
        P(DP, None),
        P(None, FS),
        P(None, FS),
        P(FS, None),
    )
    out_specs = (P(DP, FS), P())
    return jax.shard_map(local, mesh=fine, in_specs=in_specs, out_specs=out_specs, check_vma=False)
```

```python
import jax
import jax.numpy as jnp
from jax import lax
from jax.sharding import Mesh, PartitionSpec as P

EPSILON = 1e-06
FS = ("z", "ylo", "core")
DP = ("x", "yhi")


def rs_cols(part, n):
    rows, cols = part.shape
    r = part.reshape(rows, n, cols // n).transpose(1, 0, 2)
    r = lax.all_to_all(r, FS, 0, 0, tiled=False)
    return jnp.sum(r.astype(jnp.float32), 0)


def ag_cols(piece, n):
    rows, cols = piece.shape
    g = lax.all_to_all(jnp.broadcast_to(piece[None], (n, rows, cols)), FS, 0, 0, tiled=False)
    return g.transpose(1, 0, 2).reshape(rows, n * cols)


def ag_rows(piece, n):
    rows, cols = piece.shape
    g = lax.all_to_all(jnp.broadcast_to(piece[None], (n, rows, cols)), DP, 0, 0, tiled=False)
    return g.reshape(n * rows, cols)


def psum_all(x):
    for axis in ("core", "ylo", "z", "x", "yhi"):
        x = lax.psum(x, axis)
    return x


def silu_parts(preact):
    sigma = jax.nn.sigmoid(preact)
    silu_val = preact * sigma
    slope = sigma * (1.0 + preact * (1.0 - sigma))
    curve = sigma * (1.0 - sigma) * (2.0 + preact * (1.0 - 2.0 * sigma))
    return (silu_val, slope, curve)


def matmul(left, right):
    return jnp.dot(left, right, preferred_element_type=jnp.float32)


def inner_rows(left, right):
    return lax.dot_general(
        left, right, (((0,), (0,)), ((), ())), preferred_element_type=jnp.float32
    )


def inner_cols(left, right):
    return lax.dot_general(
        left, right, (((1,), (1,)), ((), ())), preferred_element_type=jnp.float32
    )


def mlp_forward(inputs, w_gate, w_up, w_down):
    gate_pre = matmul(inputs, w_gate)
    upper = matmul(inputs, w_up)
    silu_val, slope, curve = silu_parts(gate_pre)
    hidden = (silu_val * upper).astype(jnp.bfloat16)
    return (upper, silu_val, slope, curve, hidden, matmul(hidden, w_down))


def backward(inputs, labels, output, upper, silu_val, slope, w_down, token_total):
    error = (
        (inputs.astype(jnp.float32) + output - labels.astype(jnp.float32)) / token_total
    ).astype(jnp.bfloat16)
    back_hidden = inner_cols(error, w_down)
    gate_back = (back_hidden * upper * slope).astype(jnp.bfloat16)
    upper_back = (back_hidden * silu_val).astype(jnp.bfloat16)
    return (error, back_hidden, gate_back, upper_back)


def backward2(error, upper, silu_val, slope, w_down):
    back_hidden = inner_cols(error, w_down)
    gate_back = (back_hidden * upper * slope).astype(jnp.bfloat16)
    upper_back = (back_hidden * silu_val).astype(jnp.bfloat16)
    return (error, back_hidden, gate_back, upper_back)


def grad_rows(inputs, error, hidden, gate_back, upper_back):
    return jnp.concatenate(
        [inner_rows(inputs, gate_back), inner_rows(inputs, upper_back), inner_rows(error, hidden)],
        axis=1,
    )


def local(target_x, target_y, poison_x, poison_y, w_gate, w_up, w_down):
    hidden_width = w_gate.shape[1]
    model_width = w_gate.shape[0]
    dp_size = lax.axis_size(DP)
    fs_size = lax.axis_size(FS)
    tgt_total = target_x.shape[0] * dp_size
    poi_total = poison_x.shape[0] * dp_size
    upper_tgt, silu_tgt, slope_tgt, curve_tgt, hidden_tgt, part_tgt = mlp_forward(
        target_x, w_gate, w_up, w_down
    )
    upper_poi, silu_poi, slope_poi, curve_poi, hidden_poi, part_poi = mlp_forward(
        poison_x, w_gate, w_up, w_down
    )
    n_tgt = target_x.shape[0]
    fidx = lax.axis_index(FS)
    width = model_width // fs_size
    x_loc = jnp.concatenate([target_x, poison_x], 0)
    x_rows = lax.all_to_all(
        x_loc.reshape(-1, dp_size, model_width // dp_size).transpose(1, 0, 2), DP, 0, 0, tiled=False
    )
    x_rows, part_tgt, part_poi = lax.optimization_barrier((x_rows, part_tgt, part_poi))
    out_cols = rs_cols(
        jnp.concatenate([part_tgt, part_poi], axis=0).astype(jnp.bfloat16), fs_size
    )
    x_cols = lax.dynamic_slice_in_dim(jnp.concatenate([target_x, poison_x], 0), fidx * width, width, 1)
    y_cols = lax.dynamic_slice_in_dim(jnp.concatenate([target_y, poison_y], 0), fidx * width, width, 1)
    scale_rows = jnp.concatenate(
        [jnp.full((n_tgt, 1), float(tgt_total), jnp.float32),
         jnp.full((poison_x.shape[0], 1), float(poi_total), jnp.float32)], 0)
    err_cols = (
        (x_cols.astype(jnp.float32) + out_cols - y_cols.astype(jnp.float32)) / scale_rows
    ).astype(jnp.bfloat16)
    error_all = jnp.concatenate(
        [
            lax.all_gather(err_cols[:n_tgt], FS, axis=1, tiled=True),
            ag_cols(err_cols[n_tgt:], fs_size),
        ],
        0,
    )
    error_tgt, back_tgt, gback_tgt, uback_tgt = backward2(
        error_all[:n_tgt], upper_tgt, silu_tgt, slope_tgt, w_down
    )
    error_poi, back_poi, gback_poi, uback_poi = backward2(
        error_all[n_tgt:], upper_poi, silu_poi, slope_poi, w_down
    )
    n_poi = poison_x.shape[0]
    rows_d = model_width // dp_size
    e_rows = lax.all_to_all(
        error_all.reshape(-1, dp_size, rows_d).transpose(1, 0, 2), DP, 0, 0, tiled=False
    )
    h_all = lax.all_gather(jnp.concatenate([hidden_tgt, hidden_poi], 0), DP, axis=0, tiled=False)
    gu_loc = jnp.concatenate(
        [
            jnp.concatenate([gback_tgt, uback_tgt], 1),
            jnp.concatenate([gback_poi, uback_poi], 1),
        ],
        0,
    )
    gu_all = lax.all_to_all(
        jnp.broadcast_to(gu_loc[None], (dp_size,) + gu_loc.shape), DP, 0, 0, tiled=False
    )

    def block_grad(xr, er, ga, ha):
        dims = (((0, 1), (0, 1)), ((), ()))
        gu = lax.dot_general(xr, ga, dims, preferred_element_type=jnp.float32)
        dn = lax.dot_general(er, ha, dims, preferred_element_type=jnp.float32)
        return jnp.concatenate([gu, dn], 1)

    grad_tgt = block_grad(x_rows[:, :n_tgt], e_rows[:, :n_tgt], gu_all[:, :n_tgt], h_all[:, :n_tgt])
    grad_poi = block_grad(x_rows[:, n_tgt:], e_rows[:, n_tgt:], gu_all[:, n_tgt:], h_all[:, n_tgt:])
    norm_tt, norm_pp, cross_tp = psum_all(
        (jnp.sum(grad_tgt * grad_tgt), jnp.sum(grad_poi * grad_poi), jnp.sum(grad_tgt * grad_poi))
    )
    length_tgt = jnp.sqrt(norm_tt + EPSILON)
    length_poi = jnp.sqrt(norm_pp + EPSILON)
    denom = length_tgt * length_poi
    alignment = 1.0 - cross_tp / denom
    coef_tgt = -1.0 / denom
    coef_poi = cross_tp / (denom * length_poi * length_poi)
    local_sens = (coef_tgt * grad_tgt + coef_poi * grad_poi).astype(jnp.bfloat16)
    v_down = lax.all_gather(local_sens[:, 2 * hidden_width :], DP, axis=0, tiled=True)
    full_gu = ag_rows(local_sens[:, : 2 * hidden_width], dp_size)
    v_gate = full_gu[:, :hidden_width]
    v_upper = full_gu[:, hidden_width:]
    tan_gate = matmul(poison_x, v_gate)
    tan_upper = matmul(poison_x, v_upper)
    hidden_tan = (slope_poi * tan_gate * upper_poi + silu_poi * tan_upper).astype(jnp.bfloat16)
    part_tan = matmul(hidden_tan, w_down) + inner_cols(hidden_poi, v_down)
    tan_cols = rs_cols(part_tan.astype(jnp.bfloat16), fs_size)
    back_cols = (tan_cols / poi_total).astype(jnp.bfloat16)
    back_tan = ag_cols(back_cols, fs_size)
    mixed = inner_cols(back_tan, w_down) + matmul(error_poi, v_down)
    gate_total = (
        mixed * upper_poi * slope_poi
        + back_poi * (curve_poi * tan_gate * upper_poi + slope_poi * tan_upper)
    ).astype(jnp.bfloat16)
    upper_total = (mixed * silu_poi + back_poi * slope_poi * tan_gate).astype(jnp.bfloat16)
    gate_dir = (back_poi * slope_poi * upper_poi).astype(jnp.bfloat16)
    upper_dir = (back_poi * silu_poi).astype(jnp.bfloat16)
    part_grad = (
        inner_cols(gate_total, w_gate)
        + inner_cols(upper_total, w_up)
        + inner_cols(gate_dir, v_gate)
        + inner_cols(upper_dir, v_upper)
    )
    grad_cols = rs_cols(part_grad.astype(jnp.bfloat16), fs_size)
    residual_cols = back_cols.astype(jnp.float32)
    scaled = (grad_cols + residual_cols) * float(poi_total * model_width)
    total_sq = psum_all(jnp.sum(scaled * scaled))
    mean_sq = total_sq / float(poi_total * model_width)
    return (scaled * lax.rsqrt(mean_sq + EPSILON), alignment)


def solution(mesh):
    fine = Mesh(mesh.devices.reshape(4, 2, 2, 4, 2), FS + DP)
    in_specs = (
        P(DP, None),
        P(DP, None),
        P(DP, None),
        P(DP, None),
        P(None, FS),
        P(None, FS),
        P(FS, None),
    )
    out_specs = (P(DP, FS), P())
    return jax.shard_map(local, mesh=fine, in_specs=in_specs, out_specs=out_specs, check_vma=False)
```

```python
import jax
import jax.numpy as jnp
from jax import lax
from jax.sharding import Mesh, PartitionSpec as P

EPSILON = 1e-06
FS = ("z", "ylo", "core")
DP = ("x", "yhi")


def rs_cols(part, n):
    rows, cols = part.shape
    r = part.reshape(rows, n, cols // n).transpose(1, 0, 2)
    r = lax.all_to_all(r, FS, 0, 0, tiled=False)
    return jnp.sum(r.astype(jnp.float32), 0)


def ag_cols(piece, n):
    rows, cols = piece.shape
    g = lax.all_to_all(jnp.broadcast_to(piece[None], (n, rows, cols)), FS, 0, 0, tiled=False)
    return g.transpose(1, 0, 2).reshape(rows, n * cols)


def ag_rows(piece, n):
    rows, cols = piece.shape
    g = lax.all_to_all(jnp.broadcast_to(piece[None], (n, rows, cols)), DP, 0, 0, tiled=False)
    return g.reshape(n * rows, cols)


def psum_all(x):
    for axis in (("core", "ylo"), "z", "x", "yhi"):
        x = lax.psum(x, axis)
    return x


def silu_parts(preact):
    sigma = jax.nn.sigmoid(preact)
    silu_val = preact * sigma
    slope = sigma * (1.0 + preact * (1.0 - sigma))
    curve = sigma * (1.0 - sigma) * (2.0 + preact * (1.0 - 2.0 * sigma))
    return (silu_val, slope, curve)


def matmul(left, right):
    return jnp.dot(left, right, preferred_element_type=jnp.float32)


def inner_rows(left, right):
    return lax.dot_general(
        left, right, (((0,), (0,)), ((), ())), preferred_element_type=jnp.float32
    )


def inner_cols(left, right):
    return lax.dot_general(
        left, right, (((1,), (1,)), ((), ())), preferred_element_type=jnp.float32
    )


def mlp_forward(inputs, w_gate, w_up, w_down):
    gate_pre = matmul(inputs, w_gate)
    upper = matmul(inputs, w_up)
    silu_val, slope, curve = silu_parts(gate_pre)
    hidden = (silu_val * upper).astype(jnp.bfloat16)
    return (upper, silu_val, slope, curve, hidden, matmul(hidden, w_down))


def backward(inputs, labels, output, upper, silu_val, slope, w_down, token_total):
    error = (
        (inputs.astype(jnp.float32) + output - labels.astype(jnp.float32)) / token_total
    ).astype(jnp.bfloat16)
    back_hidden = inner_cols(error, w_down)
    gate_back = (back_hidden * upper * slope).astype(jnp.bfloat16)
    upper_back = (back_hidden * silu_val).astype(jnp.bfloat16)
    return (error, back_hidden, gate_back, upper_back)


def backward2(error, upper, silu_val, slope, w_down):
    back_hidden = inner_cols(error, w_down)
    gate_back = (back_hidden * upper * slope).astype(jnp.bfloat16)
    upper_back = (back_hidden * silu_val).astype(jnp.bfloat16)
    return (error, back_hidden, gate_back, upper_back)


def grad_rows(inputs, error, hidden, gate_back, upper_back):
    return jnp.concatenate(
        [inner_rows(inputs, gate_back), inner_rows(inputs, upper_back), inner_rows(error, hidden)],
        axis=1,
    )


def local(target_x, target_y, poison_x, poison_y, w_gate, w_up, w_down):
    hidden_width = w_gate.shape[1]
    model_width = w_gate.shape[0]
    dp_size = lax.axis_size(DP)
    fs_size = lax.axis_size(FS)
    tgt_total = target_x.shape[0] * dp_size
    poi_total = poison_x.shape[0] * dp_size
    upper_tgt, silu_tgt, slope_tgt, curve_tgt, hidden_tgt, part_tgt = mlp_forward(
        target_x, w_gate, w_up, w_down
    )
    upper_poi, silu_poi, slope_poi, curve_poi, hidden_poi, part_poi = mlp_forward(
        poison_x, w_gate, w_up, w_down
    )
    n_tgt = target_x.shape[0]
    fidx = lax.axis_index(FS)
    width = model_width // fs_size
    x_loc = jnp.concatenate([target_x, poison_x], 0)
    x_rows = lax.all_to_all(
        x_loc.reshape(-1, dp_size, model_width // dp_size).transpose(1, 0, 2), DP, 0, 0, tiled=False
    )
    x_rows, part_tgt, part_poi = lax.optimization_barrier((x_rows, part_tgt, part_poi))
    out_cols = rs_cols(
        jnp.concatenate([part_tgt, part_poi], axis=0).astype(jnp.bfloat16), fs_size
    )
    x_cols = lax.dynamic_slice_in_dim(jnp.concatenate([target_x, poison_x], 0), fidx * width, width, 1)
    y_cols = lax.dynamic_slice_in_dim(jnp.concatenate([target_y, poison_y], 0), fidx * width, width, 1)
    scale_rows = jnp.concatenate(
        [jnp.full((n_tgt, 1), float(tgt_total), jnp.float32),
         jnp.full((poison_x.shape[0], 1), float(poi_total), jnp.float32)], 0)
    err_cols = (
        (x_cols.astype(jnp.float32) + out_cols - y_cols.astype(jnp.float32)) / scale_rows
    ).astype(jnp.bfloat16)
    error_all = ag_cols(err_cols, fs_size)
    error_tgt, back_tgt, gback_tgt, uback_tgt = backward2(
        error_all[:n_tgt], upper_tgt, silu_tgt, slope_tgt, w_down
    )
    error_poi, back_poi, gback_poi, uback_poi = backward2(
        error_all[n_tgt:], upper_poi, silu_poi, slope_poi, w_down
    )
    n_poi = poison_x.shape[0]
    rows_d = model_width // dp_size
    e_rows = lax.all_to_all(
        error_all.reshape(-1, dp_size, rows_d).transpose(1, 0, 2), DP, 0, 0, tiled=False
    )
    h_all = lax.all_gather(jnp.concatenate([hidden_tgt, hidden_poi], 0), DP, axis=0, tiled=False)
    gu_loc = jnp.concatenate(
        [
            jnp.concatenate([gback_tgt, uback_tgt], 1),
            jnp.concatenate([gback_poi, uback_poi], 1),
        ],
        0,
    )
    gu_all = lax.all_to_all(
        jnp.broadcast_to(gu_loc[None], (dp_size,) + gu_loc.shape), DP, 0, 0, tiled=False
    )

    def block_grad(xr, er, ga, ha):
        dims = (((0, 1), (0, 1)), ((), ()))
        gu = lax.dot_general(xr, ga, dims, preferred_element_type=jnp.float32)
        dn = lax.dot_general(er, ha, dims, preferred_element_type=jnp.float32)
        return jnp.concatenate([gu, dn], 1)

    grad_tgt = block_grad(x_rows[:, :n_tgt], e_rows[:, :n_tgt], gu_all[:, :n_tgt], h_all[:, :n_tgt])
    grad_poi = block_grad(x_rows[:, n_tgt:], e_rows[:, n_tgt:], gu_all[:, n_tgt:], h_all[:, n_tgt:])
    norm_tt, norm_pp, cross_tp = psum_all(
        (jnp.sum(grad_tgt * grad_tgt), jnp.sum(grad_poi * grad_poi), jnp.sum(grad_tgt * grad_poi))
    )
    length_tgt = jnp.sqrt(norm_tt + EPSILON)
    length_poi = jnp.sqrt(norm_pp + EPSILON)
    denom = length_tgt * length_poi
    alignment = 1.0 - cross_tp / denom
    coef_tgt = -1.0 / denom
    coef_poi = cross_tp / (denom * length_poi * length_poi)
    local_sens = (coef_tgt * grad_tgt + coef_poi * grad_poi).astype(jnp.bfloat16)
    v_down = lax.all_gather(local_sens[:, 2 * hidden_width :], DP, axis=0, tiled=True)
    full_gu = ag_rows(local_sens[:, : 2 * hidden_width], dp_size)
    v_gate = full_gu[:, :hidden_width]
    v_upper = full_gu[:, hidden_width:]
    tan_gate = matmul(poison_x, v_gate)
    tan_upper = matmul(poison_x, v_upper)
    hidden_tan = (slope_poi * tan_gate * upper_poi + silu_poi * tan_upper).astype(jnp.bfloat16)
    part_tan = matmul(hidden_tan, w_down) + inner_cols(hidden_poi, v_down)
    tan_cols = rs_cols(part_tan.astype(jnp.bfloat16), fs_size)
    back_cols = (tan_cols / poi_total).astype(jnp.bfloat16)
    back_tan = ag_cols(back_cols, fs_size)
    mixed = inner_cols(back_tan, w_down) + matmul(error_poi, v_down)
    gate_total = (
        mixed * upper_poi * slope_poi
        + back_poi * (curve_poi * tan_gate * upper_poi + slope_poi * tan_upper)
    ).astype(jnp.bfloat16)
    upper_total = (mixed * silu_poi + back_poi * slope_poi * tan_gate).astype(jnp.bfloat16)
    gate_dir = (back_poi * slope_poi * upper_poi).astype(jnp.bfloat16)
    upper_dir = (back_poi * silu_poi).astype(jnp.bfloat16)
    part_grad = (
        inner_cols(gate_total, w_gate)
        + inner_cols(upper_total, w_up)
        + inner_cols(gate_dir, v_gate)
        + inner_cols(upper_dir, v_upper)
    )
    grad_cols = rs_cols(part_grad.astype(jnp.bfloat16), fs_size)
    residual_cols = back_cols.astype(jnp.float32)
    scaled = (grad_cols + residual_cols) * float(poi_total * model_width)
    total_sq = psum_all(jnp.sum(scaled * scaled))
    mean_sq = total_sq / float(poi_total * model_width)
    return (scaled * lax.rsqrt(mean_sq + EPSILON), alignment)


def solution(mesh):
    fine = Mesh(mesh.devices.reshape(4, 2, 2, 4, 2), FS + DP)
    in_specs = (
        P(DP, None),
        P(DP, None),
        P(DP, None),
        P(DP, None),
        P(None, FS),
        P(None, FS),
        P(FS, None),
    )
    out_specs = (P(DP, FS), P())
    return jax.shard_map(local, mesh=fine, in_specs=in_specs, out_specs=out_specs, check_vma=False)
```
